32 devices in a mesh: wide: 8 (over z, y), tm: 4 (over x, core).
Axes of the slice: x: 2, y: 2, z: 4, core: 2. Of those that a mesh axis runs over, the one named last changes fastest.
Arguments:
- samples: bfloat16 [32, 1024, 2048], P('tm', 'wide'), may hold values from -6 to 6
- feed_input_wiring: int32 [1024], replicated, may hold values from 0 to 1023, each once
- input_flags: int32 [1024], replicated, may hold values 0 or 1
Outputs:
- delay_spectra: float32 [4096, 2, 512], P(('wide', 'tm'))
The draws below stay inside these ranges and needn't reach their ends.
Inputs may be any that keep to these rules, and one draw needn't show every extreme that they name: `feed_input_wiring`: a permutation of the inputs.
All inputs are finite; a program needn't handle non-finite values.
Results may differ from the reference program's by a relative error of at most 0.0058.
Values may be sent and summed in bfloat16 or wider, within the bound.
No kernel may reach another device: no remote copies, remote signals or barrier semaphores. Data moves between devices by JAX's collectives and lax.ppermute only.
A program may use at most 128 MiB of HBM per device.

```python
import math
import jax
import jax.numpy as jnp
from jax import lax

CYL = 4
FEEDS = 256
NSAMP = 2048
CH = 512
CHAN_LO = 256
FRAMES = 32
INPUTS = 1024
NBASE = 4096


def plant(drawn, key, smallest, high):
    spot = [jax.random.randint(jax.random.fold_in(key, axis), (), 0, length) for axis, length in enumerate(drawn.shape)]
    main_axis = drawn.shape.index(max(drawn.shape))
    next_to = spot[:main_axis] + [(spot[main_axis] + 1) % drawn.shape[main_axis]] + spot[main_axis + 1:]
    return drawn.at[tuple(spot)].set(smallest).at[tuple(next_to)].set(high)


def block_levels(key, shape, pieces, low, top_value):
    level = 1.0
    for position, shards_of in pieces:
        draws = jax.random.uniform(jax.random.fold_in(jax.random.fold_in(key, 6), position), (shards_of,), jnp.float32, low / len(pieces), top_value / len(pieces))
        level = level * jnp.repeat(jnp.exp(draws), shape[position] // shards_of).reshape((-1,) + (1,) * (len(shape) - 1 - position))
    return level


def normal_values(key, extent, scale, bound, split=(), held_as=jnp.bfloat16):
    level = block_levels(key, extent, split, -0.22, 0.18) if split else 1.0
    values = jax.random.normal(key, extent, jnp.float32) * scale * level
    return jnp.minimum(jnp.maximum(values, -bound), bound).astype(held_as)


def setup_inputs(seed: int = 0) -> dict:
    key_of = jax.random.split(jax.random.key(seed), 4)
    return {
        "samples": normal_values(key_of[0], (FRAMES, INPUTS, NSAMP), 1.0, 6.0, ((0, 4), (1, 8))),
        "feed_input_wiring": jax.random.permutation(key_of[1], INPUTS).astype(jnp.int32),
        "input_flags": plant((jax.random.randint(key_of[2], (INPUTS,), 0, 8) < 7).astype(jnp.int32), jax.random.fold_in(key_of[2], 1), 0, 1),
    }


def channel_table(length, frequency_channels, first):
    samples_at = jnp.arange(length, dtype=jnp.int32)
    channel_at = jnp.arange(frequency_channels, dtype=jnp.int32) + first
    turns = samples_at[:, None] * channel_at[None, :] % length
    phase = turns.astype(jnp.float32) * (2.0 * math.pi / length)
    scale = 1.0 / math.sqrt(length)
    both = jnp.stack([jnp.cos(phase) * scale, -jnp.sin(phase) * scale], axis=2)
    return both.reshape(length, 2 * frequency_channels).astype(jnp.bfloat16)

def diag_sums(tiles):
    length = tiles.shape[-1]
    leading = tiles.shape[:-2]
    flattened = tiles.reshape(leading + (length * length,))
    flattened = jnp.pad(flattened, [(0, 0)] * len(leading) + [(0, length)])
    skewed = flattened.reshape(leading + (length, length + 1))[..., :length]
    row_at = jnp.arange(length, dtype=jnp.int32)[:, None]
    col_at = jnp.arange(length, dtype=jnp.int32)[None, :]
    inside = col_at < length - row_at
    return lax.optimization_barrier(jnp.sum(jnp.where(inside, skewed, jnp.zeros_like(skewed)), axis=-2))

def pair_keep():
    same = jnp.eye(CYL, dtype=jnp.float32)[:, :, None]
    first = (jnp.arange(FEEDS, dtype=jnp.int32) == 0).astype(jnp.float32)[None, None, :]
    return 1.0 - same * first

def stack_counts(feed_input_wiring, input_flags):
    placed = input_flags[feed_input_wiring].astype(jnp.float32).reshape(CYL, FEEDS)
    tiles = placed[:, None, :, None] * placed[None, :, None, :]
    return (diag_sums(tiles) * pair_keep()).reshape(NBASE)

def delay_transform(visibility_product, counts, frames_all):
    frequency_channels = visibility_product.shape[0]
    index = jnp.arange(frequency_channels, dtype=jnp.int32)
    phase = (index[:, None] * index[None, :] % frequency_channels).astype(jnp.float32) * (2.0 * math.pi / frequency_channels)
    cosine = jnp.cos(phase)
    sine = jnp.sin(phase)
    high = lax.Precision.HIGHEST
    real_part = jnp.einsum('cb,ct->bt', visibility_product[:, 0], cosine, precision=high) + jnp.einsum('cb,ct->bt', visibility_product[:, 1], sine, precision=high)
    imag_part = jnp.einsum('cb,ct->bt', visibility_product[:, 1], cosine, precision=high) - jnp.einsum('cb,ct->bt', visibility_product[:, 0], sine, precision=high)
    weight = 1.0 / jnp.sqrt(frames_all * frequency_channels * jnp.maximum(counts, 1.0))
    return jnp.stack([real_part, imag_part], axis=1) * weight[:, None, None]

def reference(samples, feed_input_wiring, input_flags):
    table = channel_table(NSAMP, CH, CHAN_LO)
    flattened = samples.reshape(FRAMES * INPUTS, NSAMP)
    spectra = lax.dot_general(table, flattened, (((0,), (1,)), ((), ())), preferred_element_type=jnp.float32)
    spectra = spectra.astype(jnp.bfloat16).reshape(CH, 2, FRAMES, INPUTS)
    spectra = spectra * input_flags.astype(jnp.bfloat16)
    spectra = jnp.take(spectra, feed_input_wiring, axis=3)
    keep = pair_keep()

    def per_channel(channel):
        wide_channel = channel.astype(jnp.float32)
        left_rows = wide_channel.reshape(2 * FRAMES, CYL, FEEDS)
        rotated = jnp.concatenate([-wide_channel[1], wide_channel[0]], axis=0).reshape(2 * FRAMES, CYL, FEEDS)
        right_rows = jnp.stack([left_rows, rotated])
        tiles = jnp.einsum('kai,ckbj->cabij', left_rows, right_rows, precision=lax.Precision.HIGHEST)
        return (diag_sums(tiles) * keep).reshape(2, NBASE)
    visibility_product = lax.map(per_channel, spectra)
    counts = stack_counts(feed_input_wiring, input_flags)
    return delay_transform(visibility_product, counts, FRAMES)
```

```python
import math

import numpy as np
import jax
import jax.numpy as jnp
from jax import lax
from jax.experimental import pallas as pl
from jax.experimental.pallas import tpu as pltpu
from jax.sharding import PartitionSpec as P

CYL = 4
FEEDS = 256
NSAMP = 2048
CH = 512
CHAN_LO = 256
NBASE = 4096

NT = (((1,), (1,)), ((), ()))


def channel_table_const(length, frequency_channels, first):
    samples_at = np.arange(length, dtype=np.int64)
    channel_at = np.arange(frequency_channels, dtype=np.int64) + first
    turns = (channel_at[:, None] * samples_at[None, :]) % length
    phase = turns.astype(np.float32) * np.float32(2.0 * math.pi / length)
    scale = np.float32(1.0 / math.sqrt(length))
    both = np.stack([np.cos(phase) * scale, -np.sin(phase) * scale], axis=1)
    return jnp.asarray(both.reshape(2 * frequency_channels, length), dtype=jnp.bfloat16)


def delay_matrix_const(frequency_channels):
    index = np.arange(frequency_channels, dtype=np.int64)
    phase = ((index[:, None] * index[None, :]) % frequency_channels).astype(np.float32) * np.float32(
        2.0 * math.pi / frequency_channels
    )
    cosine = np.cos(phase).astype(np.float32)
    sine = np.sin(phase).astype(np.float32)
    w = np.zeros((frequency_channels, 2, 2, frequency_channels), np.float32)
    w[:, 0, 0] = cosine
    w[:, 1, 0] = sine
    w[:, 0, 1] = -sine
    w[:, 1, 1] = cosine
    return jnp.asarray(w.reshape(2 * frequency_channels, 2 * frequency_channels))


def pair_keep():
    same = jnp.eye(CYL, dtype=jnp.float32)[:, :, None]
    first = (jnp.arange(FEEDS, dtype=jnp.int32) == 0).astype(jnp.float32)[None, None, :]
    return 1.0 - same * first


def stack_counts(feed_input_wiring, input_flags):
    placed = input_flags[feed_input_wiring].astype(jnp.float32).reshape(CYL, FEEDS)
    padded = jnp.pad(placed, ((0, 0), (0, FEEDS)))[:, None, :]
    kernel = placed[:, None, :]
    corr = lax.conv_general_dilated(
        padded, kernel, (1,), "VALID", dimension_numbers=("NCH", "OIH", "NCH"),
        precision=lax.Precision.HIGHEST,
    )
    counts = jnp.transpose(corr[:, :, :FEEDS], (1, 0, 2))
    return (counts * pair_keep()).reshape(NBASE)


def correlate_kernel(x_ref, pt_ref, ptr_ref, rm_ref, o_ref):
    wide_parts = x_ref.shape[0]
    g = None
    gr = None
    for w in range(wide_parts):
        xw = x_ref[w].reshape(-1, x_ref.shape[-1])
        gw = lax.dot_general(pt_ref[w], xw, NT, preferred_element_type=jnp.float32)
        grw = lax.dot_general(ptr_ref[w], xw, NT, preferred_element_type=jnp.float32)
        g = gw if g is None else g + gw
        gr = grw if gr is None else gr + grw
    g = g.astype(jnp.bfloat16)
    gr = gr.astype(jnp.bfloat16)
    yr = jnp.dot(gr, rm_ref[...], preferred_element_type=jnp.float32).astype(jnp.bfloat16)
    row_at = lax.broadcasted_iota(jnp.int32, (FEEDS, FEEDS), 0)
    col_at = lax.broadcasted_iota(jnp.int32, (FEEDS, FEEDS), 1)
    upper = col_at >= row_at
    for a in range(CYL):
        left = g[a * FEEDS:(a + 1) * FEEDS]
        for b in range(a, CYL):
            for part, right in enumerate((gr, yr)):
                tile = lax.dot_general(
                    left, right[b * FEEDS:(b + 1) * FEEDS], NT, preferred_element_type=jnp.float32
                )
                skewed = pltpu.roll(tile, 0, 1, stride=1, stride_axis=0)
                up = jnp.sum(jnp.where(upper, skewed, 0.0), axis=0, keepdims=True)
                o_ref[0, part, pl.ds(a * CYL + b, 1), :] = up
                if a < b:
                    total = jnp.sum(skewed, axis=0, keepdims=True)
                    o_ref[0, part, pl.ds(b * CYL + a, 1), :] = total - up


def correlate(blocks, pt, ptr, rm):
    wide_parts, tm_parts, local_channels, rows_each, inputs_each = blocks.shape
    return pl.pallas_call(
        correlate_kernel,
        grid=(local_channels,),
        in_specs=[
            pl.BlockSpec((wide_parts, tm_parts, None, rows_each, inputs_each), lambda c: (0, 0, c, 0, 0)),
            pl.BlockSpec(pt.shape, lambda c: (0, 0, 0)),
            pl.BlockSpec(ptr.shape, lambda c: (0, 0, 0)),
            pl.BlockSpec(rm.shape, lambda c: (0, 0)),
        ],
        out_specs=pl.BlockSpec((1, 2, CYL * CYL, FEEDS), lambda c: (c, 0, 0, 0)),
        out_shape=jax.ShapeDtypeStruct((local_channels, 2, CYL * CYL, FEEDS), jnp.float32),
    )(blocks, pt, ptr, rm)


def unskew(sums):
    sign = jnp.array([1.0, -1.0], jnp.float32)[None, :, None]
    pieces = {}
    for a in range(CYL):
        for b in range(a, CYL):
            forward = jnp.flip(sums[:, :, a * CYL + b, :], axis=-1)
            pieces[(a, b)] = forward
            if a < b:
                lower = sums[:, :, b * CYL + a, :]
                backward = jnp.concatenate([forward[:, :, :1], lower[:, :, : FEEDS - 1]], axis=-1)
                pieces[(b, a)] = backward * sign
    stacked = jnp.stack([pieces[(a, b)] for a in range(CYL) for b in range(CYL)], axis=2)
    return stacked * pair_keep().reshape(1, 1, CYL * CYL, FEEDS)


def body(samples, feed_input_wiring, input_flags):
    frames_here, inputs_here, length = samples.shape
    tm_parts = lax.axis_size("tm")
    wide_parts = lax.axis_size("wide")
    devices = tm_parts * wide_parts
    frames_all = frames_here * tm_parts
    local_channels = CH // devices
    table = channel_table_const(NSAMP, CH, CHAN_LO)
    flattened = samples.reshape(frames_here * inputs_here, length)
    spectra = lax.dot_general(table, flattened, NT, preferred_element_type=jnp.float32)
    spectra = spectra.astype(jnp.bfloat16).reshape(devices, local_channels, 2 * frames_here, inputs_here)
    turned = lax.all_to_all(spectra, ("wide", "tm"), 0, 0, tiled=True)
    blocks = turned.reshape(wide_parts, tm_parts, local_channels, 2 * frames_here, inputs_here)

    inputs_all = wide_parts * inputs_here
    flags = input_flags.astype(jnp.bfloat16)
    source = jnp.arange(inputs_all, dtype=jnp.int32)
    feed_at = jnp.arange(CYL * FEEDS, dtype=jnp.int32)
    reversed_at = (feed_at // FEEDS) * FEEDS + (FEEDS - 1 - feed_at % FEEDS)
    wiring_rev = feed_input_wiring[reversed_at]
    pt = jnp.where(feed_input_wiring[:, None] == source[None, :], flags[None, :], jnp.bfloat16(0))
    ptr = jnp.where(wiring_rev[:, None] == source[None, :], flags[None, :], jnp.bfloat16(0))
    pt = pt.reshape(CYL * FEEDS, wide_parts, inputs_here).transpose(1, 0, 2)
    ptr = ptr.reshape(CYL * FEEDS, wide_parts, inputs_here).transpose(1, 0, 2)

    rows = tm_parts * 2 * frames_here
    r_at = np.arange(rows)
    frame_at = r_at % frames_here
    part_at = (r_at // frames_here) % 2
    group_at = r_at // (2 * frames_here)
    rm = np.zeros((rows, rows), np.float32)
    for r in range(rows):
        partner = group_at[r] * 2 * frames_here + (1 - part_at[r]) * frames_here + frame_at[r]
        rm[partner, r] = -1.0 if part_at[r] == 0 else 1.0
    rm = jnp.asarray(rm, dtype=jnp.bfloat16)

    sums = correlate(blocks, pt, ptr, rm)
    partial_sums = unskew(sums).reshape(local_channels, 2, NBASE)
    visibility_product = lax.all_to_all(partial_sums, ("wide", "tm"), 2, 0, tiled=True)
    local_baselines = visibility_product.shape[2]
    device_position = lax.axis_index("wide") * tm_parts + lax.axis_index("tm")
    global_stack_counts = stack_counts(feed_input_wiring, input_flags)
    local_stack_counts = lax.dynamic_slice_in_dim(
        global_stack_counts, device_position * local_baselines, local_baselines
    )
    delay = delay_matrix_const(CH)
    stacked_in = visibility_product.reshape(CH * 2, local_baselines)
    spectra_out = lax.dot_general(
        stacked_in, delay, (((0,), (0,)), ((), ())), precision=lax.Precision.HIGHEST,
        preferred_element_type=jnp.float32,
    )
    weight = 1.0 / jnp.sqrt(frames_all * CH * jnp.maximum(local_stack_counts, 1.0))
    return spectra_out.reshape(local_baselines, 2, CH) * weight[:, None, None]


def solution(mesh):
    return jax.shard_map(
        body,
        mesh=mesh,
        in_specs=(P("tm", "wide", None), P(), P()),
        out_specs=P(("wide", "tm"), None, None),
        check_vma=False,
    )
```

```python
import math

import numpy as np
import jax
import jax.numpy as jnp
from jax import lax
from jax.experimental import pallas as pl
from jax.experimental.pallas import tpu as pltpu
from jax.sharding import PartitionSpec as P

CYL = 4
FEEDS = 256
NSAMP = 2048
CH = 512
CHAN_LO = 256
NBASE = 4096

NT = (((1,), (1,)), ((), ()))


def channel_table_const(length, frequency_channels, first):
    samples_at = np.arange(length, dtype=np.int64)
    channel_at = np.arange(frequency_channels, dtype=np.int64) + first
    turns = (channel_at[:, None] * samples_at[None, :]) % length
    phase = turns.astype(np.float32) * np.float32(2.0 * math.pi / length)
    scale = np.float32(1.0 / math.sqrt(length))
    both = np.stack([np.cos(phase) * scale, -np.sin(phase) * scale], axis=1)
    return jnp.asarray(both.reshape(2 * frequency_channels, length), dtype=jnp.bfloat16)


def delay_matrix_const(frequency_channels):
    index = np.arange(frequency_channels, dtype=np.int64)
    phase = ((index[:, None] * index[None, :]) % frequency_channels).astype(np.float32) * np.float32(
        2.0 * math.pi / frequency_channels
    )
    cosine = np.cos(phase).astype(np.float32)
    sine = np.sin(phase).astype(np.float32)
    w = np.zeros((frequency_channels, 2, 2, frequency_channels), np.float32)
    w[:, 0, 0] = cosine
    w[:, 1, 0] = sine
    w[:, 0, 1] = -sine
    w[:, 1, 1] = cosine
    return jnp.asarray(w.reshape(2 * frequency_channels, 2 * frequency_channels))


def pair_keep():
    same = jnp.eye(CYL, dtype=jnp.float32)[:, :, None]
    first = (jnp.arange(FEEDS, dtype=jnp.int32) == 0).astype(jnp.float32)[None, None, :]
    return 1.0 - same * first


def diag_pairs(left, right, upper, write):
    for a in range(CYL):
        for b in range(a, CYL):
            tile = lax.dot_general(
                left[a * FEEDS:(a + 1) * FEEDS], right[b * FEEDS:(b + 1) * FEEDS], NT,
                preferred_element_type=jnp.float32,
            )
            skewed = pltpu.roll(tile, 0, 1, stride=1, stride_axis=0)
            up = jnp.sum(jnp.where(upper, skewed, 0.0), axis=0, keepdims=True)
            write(a * CYL + b, up)
            if a < b:
                total = jnp.sum(skewed, axis=0, keepdims=True)
                write(b * CYL + a, total - up)


def correlate_kernel(x_ref, pt_ref, ptr_ref, rm_ref, fm_ref, fmr_ref, o_ref, n_ref):
    wide_parts = x_ref.shape[0]
    row_at = lax.broadcasted_iota(jnp.int32, (FEEDS, FEEDS), 0)
    col_at = lax.broadcasted_iota(jnp.int32, (FEEDS, FEEDS), 1)
    upper = col_at >= row_at

    @pl.when(pl.program_id(0) == 0)
    def _():
        def write_count(slot, value):
            n_ref[pl.ds(slot, 1), :] = value

        diag_pairs(fm_ref[...], fmr_ref[...], upper, write_count)

    g = None
    gr = None
    for w in range(wide_parts):
        xw = x_ref[w].reshape(-1, x_ref.shape[-1])
        gw = lax.dot_general(pt_ref[w], xw, NT, preferred_element_type=jnp.float32)
        grw = lax.dot_general(ptr_ref[w], xw, NT, preferred_element_type=jnp.float32)
        g = gw if g is None else g + gw
        gr = grw if gr is None else gr + grw
    g = g.astype(jnp.bfloat16)
    gr = gr.astype(jnp.bfloat16)
    yr = jnp.dot(gr, rm_ref[...], preferred_element_type=jnp.float32).astype(jnp.bfloat16)
    for part, right in enumerate((gr, yr)):
        def write_vis(slot, value, part=part):
            o_ref[0, part, pl.ds(slot, 1), :] = value

        diag_pairs(g, right, upper, write_vis)


def correlate(blocks, pt, ptr, rm, fm, fmr):
    wide_parts, tm_parts, local_channels, rows_each, inputs_each = blocks.shape
    return pl.pallas_call(
        correlate_kernel,
        grid=(local_channels,),
        in_specs=[
            pl.BlockSpec((wide_parts, tm_parts, None, rows_each, inputs_each), lambda c: (0, 0, c, 0, 0)),
            pl.BlockSpec(pt.shape, lambda c: (0, 0, 0)),
            pl.BlockSpec(ptr.shape, lambda c: (0, 0, 0)),
            pl.BlockSpec(rm.shape, lambda c: (0, 0)),
            pl.BlockSpec(fm.shape, lambda c: (0, 0)),
            pl.BlockSpec(fmr.shape, lambda c: (0, 0)),
        ],
        out_specs=[
            pl.BlockSpec((1, 2, CYL * CYL, FEEDS), lambda c: (c, 0, 0, 0)),
            pl.BlockSpec((CYL * CYL, FEEDS), lambda c: (0, 0)),
        ],
        out_shape=[
            jax.ShapeDtypeStruct((local_channels, 2, CYL * CYL, FEEDS), jnp.float32),
            jax.ShapeDtypeStruct((CYL * CYL, FEEDS), jnp.float32),
        ],
    )(blocks, pt, ptr, rm, fm, fmr)


def unskew(sums, sign):
    pieces = {}
    for a in range(CYL):
        for b in range(a, CYL):
            forward = jnp.flip(sums[..., a * CYL + b, :], axis=-1)
            pieces[(a, b)] = forward
            if a < b:
                lower = sums[..., b * CYL + a, :]
                backward = jnp.concatenate([forward[..., :1], lower[..., : FEEDS - 1]], axis=-1)
                pieces[(b, a)] = backward * sign
    stacked = jnp.stack([pieces[(a, b)] for a in range(CYL) for b in range(CYL)], axis=-2)
    return stacked * pair_keep().reshape(CYL * CYL, FEEDS)


def body(samples, feed_input_wiring, input_flags):
    frames_here, inputs_here, length = samples.shape
    tm_parts = lax.axis_size("tm")
    wide_parts = lax.axis_size("wide")
    devices = tm_parts * wide_parts
    frames_all = frames_here * tm_parts
    local_channels = CH // devices
    table = channel_table_const(NSAMP, CH, CHAN_LO)
    flattened = samples.reshape(frames_here * inputs_here, length)
    spectra = lax.dot_general(table, flattened, NT, preferred_element_type=jnp.float32)
    spectra = spectra.astype(jnp.bfloat16).reshape(devices, local_channels, 2 * frames_here, inputs_here)
    turned = lax.all_to_all(spectra, ("wide", "tm"), 0, 0, tiled=True)
    blocks = turned.reshape(wide_parts, tm_parts, local_channels, 2 * frames_here, inputs_here)

    inputs_all = wide_parts * inputs_here
    flags = input_flags.astype(jnp.bfloat16)
    source = jnp.arange(inputs_all, dtype=jnp.int32)
    wiring_rev = jnp.flip(feed_input_wiring.reshape(CYL, FEEDS), axis=1).reshape(CYL * FEEDS)
    pt_full = jnp.where(feed_input_wiring[:, None] == source[None, :], flags[None, :], jnp.bfloat16(0))
    ptr_full = jnp.where(wiring_rev[:, None] == source[None, :], flags[None, :], jnp.bfloat16(0))
    first_lane = (lax.broadcasted_iota(jnp.int32, (CYL * FEEDS, 128), 1) == 0).astype(jnp.bfloat16)
    fm = jnp.sum(pt_full.astype(jnp.float32), axis=1).astype(jnp.bfloat16)[:, None] * first_lane
    fmr = jnp.sum(ptr_full.astype(jnp.float32), axis=1).astype(jnp.bfloat16)[:, None] * first_lane
    pt = pt_full.reshape(CYL * FEEDS, wide_parts, inputs_here).transpose(1, 0, 2)
    ptr = ptr_full.reshape(CYL * FEEDS, wide_parts, inputs_here).transpose(1, 0, 2)

    rows = tm_parts * 2 * frames_here
    r_at = np.arange(rows)
    frame_at = r_at % frames_here
    part_at = (r_at // frames_here) % 2
    group_at = r_at // (2 * frames_here)
    rm = np.zeros((rows, rows), np.float32)
    for r in range(rows):
        partner = group_at[r] * 2 * frames_here + (1 - part_at[r]) * frames_here + frame_at[r]
        rm[partner, r] = -1.0 if part_at[r] == 0 else 1.0
    rm = jnp.asarray(rm, dtype=jnp.bfloat16)

    sums, count_sums = correlate(blocks, pt, ptr, rm, fm, fmr)
    conj_sign = jnp.array([1.0, -1.0], jnp.float32)[None, :, None]
    vis = unskew(sums, conj_sign)
    local_baselines = NBASE // devices
    send = vis.reshape(local_channels, 2, devices, local_baselines).transpose(2, 0, 1, 3)
    received = lax.all_to_all(send, ("wide", "tm"), 0, 0, tiled=True)
    stacked_in = received.reshape(CH * 2, local_baselines)
    device_position = lax.axis_index("wide") * tm_parts + lax.axis_index("tm")
    global_stack_counts = unskew(count_sums, 1.0).reshape(NBASE)
    local_stack_counts = lax.dynamic_slice_in_dim(
        global_stack_counts, device_position * local_baselines, local_baselines
    )
    delay = delay_matrix_const(CH)
    spectra_out = lax.dot_general(
        stacked_in, delay, (((0,), (0,)), ((), ())), precision=lax.Precision.HIGHEST,
        preferred_element_type=jnp.float32,
    )
    weight = 1.0 / jnp.sqrt(frames_all * CH * jnp.maximum(local_stack_counts, 1.0))
    return spectra_out.reshape(local_baselines, 2, CH) * weight[:, None, None]


def solution(mesh):
    return jax.shard_map(
        body,
        mesh=mesh,
        in_specs=(P("tm", "wide", None), P(), P()),
        out_specs=P(("wide", "tm"), None, None),
        check_vma=False,
    )
```

```python
import functools
import math

import numpy as np
import jax
import jax.numpy as jnp
from jax import lax
from jax.experimental import pallas as pl
from jax.experimental.pallas import tpu as pltpu
from jax.sharding import PartitionSpec as P

CYL = 4
FEEDS = 256
NSAMP = 2048
CH = 512
CHAN_LO = 256
NBASE = 4096

NT = (((1,), (1,)), ((), ()))


def channel_table_const(length, frequency_channels, first):
    samples_at = np.arange(length, dtype=np.int64)
    channel_at = np.arange(frequency_channels, dtype=np.int64) + first
    turns = (channel_at[:, None] * samples_at[None, :]) % length
    phase = turns.astype(np.float32) * np.float32(2.0 * math.pi / length)
    scale = np.float32(1.0 / math.sqrt(length))
    both = np.stack([np.cos(phase) * scale, -np.sin(phase) * scale], axis=1)
    return both.reshape(2 * frequency_channels, length)


def delay_matrix_const(frequency_channels):
    index = np.arange(frequency_channels, dtype=np.int64)
    phase = ((index[:, None] * index[None, :]) % frequency_channels).astype(np.float32) * np.float32(
        2.0 * math.pi / frequency_channels
    )
    cosine = np.cos(phase).astype(np.float32)
    sine = np.sin(phase).astype(np.float32)
    w = np.zeros((frequency_channels, 2, 2, frequency_channels), np.float32)
    w[:, 0, 0] = cosine
    w[:, 1, 0] = sine
    w[:, 0, 1] = -sine
    w[:, 1, 1] = cosine
    return jnp.asarray(w.reshape(2 * frequency_channels, 2 * frequency_channels))


def pair_keep():
    same = jnp.eye(CYL, dtype=jnp.float32)[:, :, None]
    first = (jnp.arange(FEEDS, dtype=jnp.int32) == 0).astype(jnp.float32)[None, None, :]
    return 1.0 - same * first


def diag_pairs(left, right, upper, write):
    for a in range(CYL):
        for b in range(a, CYL):
            tile = lax.dot_general(
                left[a * FEEDS:(a + 1) * FEEDS], right[b * FEEDS:(b + 1) * FEEDS], NT,
                preferred_element_type=jnp.float32,
            )
            skewed = pltpu.roll(tile, 0, 1, stride=1, stride_axis=0)
            up = jnp.sum(jnp.where(upper, skewed, 0.0), axis=0, keepdims=True)
            write(a * CYL + b, up)
            if a < b:
                total = jnp.sum(skewed, axis=0, keepdims=True)
                write(b * CYL + a, total - up)


def correlate_kernel(*refs, with_counts):
    if with_counts:
        x_ref, pt_ref, ptr_ref, rm_ref, fm_ref, fmr_ref, o_ref, n_ref = refs
    else:
        x_ref, pt_ref, ptr_ref, rm_ref, o_ref = refs
    wide_parts = x_ref.shape[0]
    row_at = lax.broadcasted_iota(jnp.int32, (FEEDS, FEEDS), 0)
    col_at = lax.broadcasted_iota(jnp.int32, (FEEDS, FEEDS), 1)
    upper = col_at >= row_at

    if with_counts:
        @pl.when(pl.program_id(0) == 0)
        def _():
            def write_count(slot, value):
                n_ref[pl.ds(slot, 1), :] = value

            diag_pairs(fm_ref[...], fmr_ref[...], upper, write_count)

    g = None
    gr = None
    for w in range(wide_parts):
        xw = x_ref[w].reshape(-1, x_ref.shape[-1])
        gw = lax.dot_general(pt_ref[w], xw, NT, preferred_element_type=jnp.float32)
        grw = lax.dot_general(ptr_ref[w], xw, NT, preferred_element_type=jnp.float32)
        g = gw if g is None else g + gw
        gr = grw if gr is None else gr + grw
    g = g.astype(jnp.bfloat16)
    gr = gr.astype(jnp.bfloat16)
    yr = jnp.dot(gr, rm_ref[...], preferred_element_type=jnp.float32).astype(jnp.bfloat16)
    for part, right in enumerate((gr, yr)):
        def write_vis(slot, value, part=part):
            o_ref[0, part, pl.ds(slot, 1), :] = value

        diag_pairs(g, right, upper, write_vis)


def correlate(blocks, pt, ptr, rm, fm=None, fmr=None):
    wide_parts, tm_parts, local_channels, rows_each, inputs_each = blocks.shape
    with_counts = fm is not None
    in_specs = [
        pl.BlockSpec((wide_parts, tm_parts, None, rows_each, inputs_each), lambda c: (0, 0, c, 0, 0)),
        pl.BlockSpec(pt.shape, lambda c: (0, 0, 0)),
        pl.BlockSpec(ptr.shape, lambda c: (0, 0, 0)),
        pl.BlockSpec(rm.shape, lambda c: (0, 0)),
    ]
    out_specs = [pl.BlockSpec((1, 2, CYL * CYL, FEEDS), lambda c: (c, 0, 0, 0))]
    out_shape = [jax.ShapeDtypeStruct((local_channels, 2, CYL * CYL, FEEDS), jnp.float32)]
    operands = [blocks, pt, ptr, rm]
    if with_counts:
        in_specs += [pl.BlockSpec(fm.shape, lambda c: (0, 0)), pl.BlockSpec(fmr.shape, lambda c: (0, 0))]
        out_specs.append(pl.BlockSpec((CYL * CYL, FEEDS), lambda c: (0, 0)))
        out_shape.append(jax.ShapeDtypeStruct((CYL * CYL, FEEDS), jnp.float32))
        operands += [fm, fmr]
    positions = CYL * FEEDS
    rows = tm_parts * rows_each
    flops = local_channels * (
        2 * 2 * positions * wide_parts * inputs_each * rows + 2 * positions * rows * rows
        + 20 * 2 * FEEDS * FEEDS * rows
    )
    bytes_accessed = blocks.size * 2 + pt.size * 4 + local_channels * 2 * CYL * CYL * FEEDS * 4
    return pl.pallas_call(
        functools.partial(correlate_kernel, with_counts=with_counts),
        grid=(local_channels,),
        in_specs=in_specs,
        out_specs=out_specs,
        out_shape=out_shape,
        cost_estimate=pl.CostEstimate(flops=flops, transcendentals=0, bytes_accessed=bytes_accessed),
    )(*operands)


def unskew(sums, sign):
    pieces = {}
    for a in range(CYL):
        for b in range(a, CYL):
            forward = jnp.flip(sums[..., a * CYL + b, :], axis=-1)
            pieces[(a, b)] = forward
            if a < b:
                lower = sums[..., b * CYL + a, :]
                backward = jnp.concatenate([forward[..., :1], lower[..., : FEEDS - 1]], axis=-1)
                pieces[(b, a)] = backward * sign
    stacked = jnp.stack([pieces[(a, b)] for a in range(CYL) for b in range(CYL)], axis=-2)
    return stacked * pair_keep().reshape(CYL * CYL, FEEDS)


def body(samples, feed_input_wiring, input_flags):
    frames_here, inputs_here, length = samples.shape
    tm_parts = lax.axis_size("tm")
    wide_parts = lax.axis_size("wide")
    devices = tm_parts * wide_parts
    frames_all = frames_here * tm_parts
    local_channels = CH // devices
    table = channel_table_const(NSAMP, CH, CHAN_LO)
    chunks = math.gcd(4, local_channels)
    chunk_channels = local_channels // chunks
    table = table.reshape(devices, chunks, chunk_channels * 2, length).transpose(1, 0, 2, 3)
    table = jnp.asarray(table.reshape(chunks, devices * chunk_channels * 2, length), dtype=jnp.bfloat16)
    flattened = samples.reshape(frames_here * inputs_here, length)
    chunk_blocks = []
    for j in range(chunks):
        spectra = lax.dot_general(table[j], flattened, NT, preferred_element_type=jnp.float32)
        spectra = spectra.astype(jnp.bfloat16).reshape(devices, chunk_channels, 2 * frames_here, inputs_here)
        turned = lax.all_to_all(spectra, ("wide", "tm"), 0, 0, tiled=True)
        chunk_blocks.append(
            turned.reshape(wide_parts, tm_parts, chunk_channels, 2 * frames_here, inputs_here)
        )

    inputs_all = wide_parts * inputs_here
    flags = input_flags.astype(jnp.bfloat16)
    source = jnp.arange(inputs_all, dtype=jnp.int32)
    wiring_rev = jnp.flip(feed_input_wiring.reshape(CYL, FEEDS), axis=1).reshape(CYL * FEEDS)
    pt_full = jnp.where(feed_input_wiring[:, None] == source[None, :], flags[None, :], jnp.bfloat16(0))
    ptr_full = jnp.where(wiring_rev[:, None] == source[None, :], flags[None, :], jnp.bfloat16(0))
    first_lane = (lax.broadcasted_iota(jnp.int32, (CYL * FEEDS, 128), 1) == 0).astype(jnp.bfloat16)
    fm = jnp.sum(pt_full.astype(jnp.float32), axis=1).astype(jnp.bfloat16)[:, None] * first_lane
    fmr = jnp.sum(ptr_full.astype(jnp.float32), axis=1).astype(jnp.bfloat16)[:, None] * first_lane
    pt = pt_full.reshape(CYL * FEEDS, wide_parts, inputs_here).transpose(1, 0, 2)
    ptr = ptr_full.reshape(CYL * FEEDS, wide_parts, inputs_here).transpose(1, 0, 2)

    rows = tm_parts * 2 * frames_here
    r_at = np.arange(rows)
    frame_at = r_at % frames_here
    part_at = (r_at // frames_here) % 2
    group_at = r_at // (2 * frames_here)
    rm = np.zeros((rows, rows), np.float32)
    for r in range(rows):
        partner = group_at[r] * 2 * frames_here + (1 - part_at[r]) * frames_here + frame_at[r]
        rm[partner, r] = -1.0 if part_at[r] == 0 else 1.0
    rm = jnp.asarray(rm, dtype=jnp.bfloat16)

    sums, count_sums = correlate(chunk_blocks[0], pt, ptr, rm, fm, fmr)
    sums = [sums] + [correlate(blk, pt, ptr, rm)[0] for blk in chunk_blocks[1:]]
    sums = jnp.concatenate(sums, axis=0)
    conj_sign = jnp.array([1.0, -1.0], jnp.float32)[None, :, None]
    vis = unskew(sums, conj_sign)
    local_baselines = NBASE // devices
    send = vis.reshape(local_channels, 2, devices, local_baselines).transpose(2, 0, 1, 3)
    received = lax.all_to_all(send, ("wide", "tm"), 0, 0, tiled=True)
    stacked_in = received.reshape(CH * 2, local_baselines)
    device_position = lax.axis_index("wide") * tm_parts + lax.axis_index("tm")
    global_stack_counts = unskew(count_sums, 1.0).reshape(NBASE)
    local_stack_counts = lax.dynamic_slice_in_dim(
        global_stack_counts, device_position * local_baselines, local_baselines
    )
    delay = delay_matrix_const(CH)
    spectra_out = lax.dot_general(
        stacked_in, delay, (((0,), (0,)), ((), ())), precision=lax.Precision.HIGHEST,
        preferred_element_type=jnp.float32,
    )
    weight = 1.0 / jnp.sqrt(frames_all * CH * jnp.maximum(local_stack_counts, 1.0))
    return spectra_out.reshape(local_baselines, 2, CH) * weight[:, None, None]


def solution(mesh):
    return jax.shard_map(
        body,
        mesh=mesh,
        in_specs=(P("tm", "wide", None), P(), P()),
        out_specs=P(("wide", "tm"), None, None),
        check_vma=False,
    )
```

```python
import functools
import math

import numpy as np
import jax
import jax.numpy as jnp
from jax import lax
from jax.experimental import pallas as pl
from jax.experimental.pallas import tpu as pltpu
from jax.sharding import PartitionSpec as P

CYL = 4
FEEDS = 256
NSAMP = 2048
CH = 512
CHAN_LO = 256
NBASE = 4096

NT = (((1,), (1,)), ((), ()))


def channel_table_const(length, frequency_channels, first):
    samples_at = np.arange(length, dtype=np.int64)
    channel_at = np.arange(frequency_channels, dtype=np.int64) + first
    turns = (channel_at[:, None] * samples_at[None, :]) % length
    phase = turns.astype(np.float32) * np.float32(2.0 * math.pi / length)
    scale = np.float32(1.0 / math.sqrt(length))
    both = np.stack([np.cos(phase) * scale, -np.sin(phase) * scale], axis=1)
    return both.reshape(2 * frequency_channels, length)


def delay_matrix_const(frequency_channels):
    index = np.arange(frequency_channels, dtype=np.int64)
    phase = ((index[:, None] * index[None, :]) % frequency_channels).astype(np.float32) * np.float32(
        2.0 * math.pi / frequency_channels
    )
    cosine = np.cos(phase).astype(np.float32)
    sine = np.sin(phase).astype(np.float32)
    w = np.zeros((frequency_channels, 2, 2, frequency_channels), np.float32)
    w[:, 0, 0] = cosine
    w[:, 1, 0] = sine
    w[:, 0, 1] = -sine
    w[:, 1, 1] = cosine
    return jnp.asarray(w.reshape(2 * frequency_channels, 2 * frequency_channels))


def pair_keep():
    same = jnp.eye(CYL, dtype=jnp.float32)[:, :, None]
    first = (jnp.arange(FEEDS, dtype=jnp.int32) == 0).astype(jnp.float32)[None, None, :]
    return 1.0 - same * first


def diag_pairs(left, right, upper, write):
    for a in range(CYL):
        for b in range(a, CYL):
            tile = lax.dot_general(
                left[a * FEEDS:(a + 1) * FEEDS], right[b * FEEDS:(b + 1) * FEEDS], NT,
                preferred_element_type=jnp.float32,
            )
            skewed = pltpu.roll(tile, 0, 1, stride=1, stride_axis=0)
            up = jnp.sum(jnp.where(upper, skewed, 0.0), axis=0, keepdims=True)
            write(a * CYL + b, up)
            if a < b:
                total = jnp.sum(skewed, axis=0, keepdims=True)
                write(b * CYL + a, total - up)


def correlate_kernel(*refs, with_counts):
    if with_counts:
        x_ref, pt_ref, ptr_ref, rm_ref, fm_ref, fmr_ref, o_ref, n_ref = refs
    else:
        x_ref, pt_ref, ptr_ref, rm_ref, o_ref = refs
    wide_parts = x_ref.shape[0]
    row_at = lax.broadcasted_iota(jnp.int32, (FEEDS, FEEDS), 0)
    col_at = lax.broadcasted_iota(jnp.int32, (FEEDS, FEEDS), 1)
    upper = col_at >= row_at

    if with_counts:
        @pl.when(pl.program_id(0) == 0)
        def _():
            def write_count(slot, value):
                n_ref[pl.ds(slot, 1), :] = value

            diag_pairs(fm_ref[...], fmr_ref[...], upper, write_count)

    g = None
    gr = None
    for w in range(wide_parts):
        xw = x_ref[w].reshape(-1, x_ref.shape[-1])
        gw = lax.dot_general(pt_ref[w], xw, NT, preferred_element_type=jnp.float32)
        grw = lax.dot_general(ptr_ref[w], xw, NT, preferred_element_type=jnp.float32)
        g = gw if g is None else g + gw
        gr = grw if gr is None else gr + grw
    g = g.astype(jnp.bfloat16)
    gr = gr.astype(jnp.bfloat16)
    yr = jnp.dot(gr, rm_ref[...], preferred_element_type=jnp.float32).astype(jnp.bfloat16)
    for part, right in enumerate((gr, yr)):
        def write_vis(slot, value, part=part):
            o_ref[0, part, pl.ds(slot, 1), :] = value

        diag_pairs(g, right, upper, write_vis)


def correlate(blocks, pt, ptr, rm, fm=None, fmr=None):
    wide_parts, tm_parts, local_channels, rows_each, inputs_each = blocks.shape
    with_counts = fm is not None
    in_specs = [
        pl.BlockSpec((wide_parts, tm_parts, None, rows_each, inputs_each), lambda c: (0, 0, c, 0, 0)),
        pl.BlockSpec(pt.shape, lambda c: (0, 0, 0)),
        pl.BlockSpec(ptr.shape, lambda c: (0, 0, 0)),
        pl.BlockSpec(rm.shape, lambda c: (0, 0)),
    ]
    out_specs = [pl.BlockSpec((1, 2, CYL * CYL, FEEDS), lambda c: (c, 0, 0, 0))]
    out_shape = [jax.ShapeDtypeStruct((local_channels, 2, CYL * CYL, FEEDS), jnp.float32)]
    operands = [blocks, pt, ptr, rm]
    if with_counts:
        in_specs += [pl.BlockSpec(fm.shape, lambda c: (0, 0)), pl.BlockSpec(fmr.shape, lambda c: (0, 0))]
        out_specs.append(pl.BlockSpec((CYL * CYL, FEEDS), lambda c: (0, 0)))
        out_shape.append(jax.ShapeDtypeStruct((CYL * CYL, FEEDS), jnp.float32))
        operands += [fm, fmr]
    positions = CYL * FEEDS
    rows = tm_parts * rows_each
    flops = local_channels * (
        2 * 2 * positions * wide_parts * inputs_each * rows + 2 * positions * rows * rows
        + 20 * 2 * FEEDS * FEEDS * rows
    )
    bytes_accessed = blocks.size * 2 + pt.size * 4 + local_channels * 2 * CYL * CYL * FEEDS * 4
    return pl.pallas_call(
        functools.partial(correlate_kernel, with_counts=with_counts),
        grid=(local_channels,),
        in_specs=in_specs,
        out_specs=out_specs,
        out_shape=out_shape,
        cost_estimate=pl.CostEstimate(flops=flops, transcendentals=0, bytes_accessed=bytes_accessed),
    )(*operands)


def unskew(sums, sign):
    pieces = {}
    for a in range(CYL):
        for b in range(a, CYL):
            forward = jnp.flip(sums[..., a * CYL + b, :], axis=-1)
            pieces[(a, b)] = forward
            if a < b:
                lower = sums[..., b * CYL + a, :]
                backward = jnp.concatenate([forward[..., :1], lower[..., : FEEDS - 1]], axis=-1)
                pieces[(b, a)] = backward * sign
    stacked = jnp.stack([pieces[(a, b)] for a in range(CYL) for b in range(CYL)], axis=-2)
    return stacked * pair_keep().reshape(CYL * CYL, FEEDS)


def body(samples, feed_input_wiring, input_flags):
    frames_here, inputs_here, length = samples.shape
    tm_parts = lax.axis_size("tm")
    wide_parts = lax.axis_size("wide")
    devices = tm_parts * wide_parts
    frames_all = frames_here * tm_parts
    local_channels = CH // devices
    table = channel_table_const(NSAMP, CH, CHAN_LO)
    chunks = math.gcd(4, local_channels)
    chunk_channels = local_channels // chunks
    table = table.reshape(devices, chunks, chunk_channels * 2, length).transpose(1, 0, 2, 3)
    table = jnp.asarray(table.reshape(chunks, devices * chunk_channels * 2, length), dtype=jnp.bfloat16)
    flattened = samples.reshape(frames_here * inputs_here, length)
    spectra = lax.dot_general(
        table.reshape(chunks * devices * chunk_channels * 2, length), flattened, NT,
        preferred_element_type=jnp.float32,
    )
    spectra = spectra.astype(jnp.bfloat16).reshape(
        chunks, devices, chunk_channels, 2 * frames_here, inputs_here
    )

    inputs_all = wide_parts * inputs_here
    flags = input_flags.astype(jnp.bfloat16)
    source = jnp.arange(inputs_all, dtype=jnp.int32)
    wiring_rev = jnp.flip(feed_input_wiring.reshape(CYL, FEEDS), axis=1).reshape(CYL * FEEDS)
    pt_full = jnp.where(feed_input_wiring[:, None] == source[None, :], flags[None, :], jnp.bfloat16(0))
    ptr_full = jnp.where(wiring_rev[:, None] == source[None, :], flags[None, :], jnp.bfloat16(0))
    first_lane = (lax.broadcasted_iota(jnp.int32, (CYL * FEEDS, 128), 1) == 0).astype(jnp.bfloat16)
    fm = jnp.sum(pt_full.astype(jnp.float32), axis=1).astype(jnp.bfloat16)[:, None] * first_lane
    fmr = jnp.sum(ptr_full.astype(jnp.float32), axis=1).astype(jnp.bfloat16)[:, None] * first_lane
    pt = pt_full.reshape(CYL * FEEDS, wide_parts, inputs_here).transpose(1, 0, 2)
    ptr = ptr_full.reshape(CYL * FEEDS, wide_parts, inputs_here).transpose(1, 0, 2)

    rows = tm_parts * 2 * frames_here
    r_at = np.arange(rows)
    frame_at = r_at % frames_here
    part_at = (r_at // frames_here) % 2
    group_at = r_at // (2 * frames_here)
    rm = np.zeros((rows, rows), np.float32)
    for r in range(rows):
        partner = group_at[r] * 2 * frames_here + (1 - part_at[r]) * frames_here + frame_at[r]
        rm[partner, r] = -1.0 if part_at[r] == 0 else 1.0
    rm = jnp.asarray(rm, dtype=jnp.bfloat16)

    sums = []
    for j in range(chunks):
        spectra_j = spectra[j]
        if j >= 2:
            spectra_j, _ = lax.optimization_barrier((spectra_j, sums[j - 2]))
        turned = lax.all_to_all(spectra_j, ("wide", "tm"), 0, 0, tiled=True)
        blk = turned.reshape(wide_parts, tm_parts, chunk_channels, 2 * frames_here, inputs_here)
        if j == 0:
            first, count_sums = correlate(blk, pt, ptr, rm, fm, fmr)
            sums.append(first)
        else:
            sums.append(correlate(blk, pt, ptr, rm)[0])
    sums = jnp.concatenate(sums, axis=0)
    conj_sign = jnp.array([1.0, -1.0], jnp.float32)[None, :, None]
    vis = unskew(sums, conj_sign)
    local_baselines = NBASE // devices
    send = vis.reshape(local_channels, 2, devices, local_baselines).transpose(2, 0, 1, 3)
    received = lax.all_to_all(send, ("wide", "tm"), 0, 0, tiled=True)
    stacked_in = received.reshape(CH * 2, local_baselines)
    device_position = lax.axis_index("wide") * tm_parts + lax.axis_index("tm")
    global_stack_counts = unskew(count_sums, 1.0).reshape(NBASE)
    local_stack_counts = lax.dynamic_slice_in_dim(
        global_stack_counts, device_position * local_baselines, local_baselines
    )
    delay = delay_matrix_const(CH)
    spectra_out = lax.dot_general(
        stacked_in, delay, (((0,), (0,)), ((), ())), precision=lax.Precision.HIGHEST,
        preferred_element_type=jnp.float32,
    )
    weight = 1.0 / jnp.sqrt(frames_all * CH * jnp.maximum(local_stack_counts, 1.0))
    return spectra_out.reshape(local_baselines, 2, CH) * weight[:, None, None]


def solution(mesh):
    return jax.shard_map(
        body,
        mesh=mesh,
        in_specs=(P("tm", "wide", None), P(), P()),
        out_specs=P(("wide", "tm"), None, None),
        check_vma=False,
    )
```

```python
import functools
import math

import numpy as np
import jax
import jax.numpy as jnp
from jax import lax
from jax.experimental import pallas as pl
from jax.experimental.pallas import tpu as pltpu
from jax.sharding import PartitionSpec as P

CYL = 4
FEEDS = 256
NSAMP = 2048
CH = 512
CHAN_LO = 256
NBASE = 4096

NT = (((1,), (1,)), ((), ()))


def channel_table_const(length, frequency_channels, first):
    samples_at = np.arange(length, dtype=np.int64)
    channel_at = np.arange(frequency_channels, dtype=np.int64) + first
    turns = (channel_at[:, None] * samples_at[None, :]) % length
    phase = turns.astype(np.float32) * np.float32(2.0 * math.pi / length)
    scale = np.float32(1.0 / math.sqrt(length))
    both = np.stack([np.cos(phase) * scale, -np.sin(phase) * scale], axis=1)
    return both.reshape(2 * frequency_channels, length)


def delay_matrix_const(frequency_channels):
    index = np.arange(frequency_channels, dtype=np.int64)
    phase = ((index[:, None] * index[None, :]) % frequency_channels).astype(np.float32) * np.float32(
        2.0 * math.pi / frequency_channels
    )
    cosine = np.cos(phase).astype(np.float32)
    sine = np.sin(phase).astype(np.float32)
    w = np.zeros((frequency_channels, 2, 2, frequency_channels), np.float32)
    w[:, 0, 0] = cosine
    w[:, 1, 0] = sine
    w[:, 0, 1] = -sine
    w[:, 1, 1] = cosine
    return jnp.asarray(w.reshape(2 * frequency_channels, 2 * frequency_channels))


def pair_keep():
    same = jnp.eye(CYL, dtype=jnp.float32)[:, :, None]
    first = (jnp.arange(FEEDS, dtype=jnp.int32) == 0).astype(jnp.float32)[None, None, :]
    return 1.0 - same * first


def diag_pairs(left, right, upper, write):
    for a in range(CYL):
        for b in range(a, CYL):
            tile = lax.dot_general(
                left[a * FEEDS:(a + 1) * FEEDS], right[b * FEEDS:(b + 1) * FEEDS], NT,
                preferred_element_type=jnp.float32,
            )
            skewed = pltpu.roll(tile, 0, 1, stride=1, stride_axis=0)
            up = jnp.sum(jnp.where(upper, skewed, 0.0), axis=0, keepdims=True)
            write(a * CYL + b, up)
            if a < b:
                total = jnp.sum(skewed, axis=0, keepdims=True)
                write(b * CYL + a, total - up)


def correlate_kernel(*refs, with_counts):
    if with_counts:
        x_ref, pt_ref, ptr_ref, rm_ref, fm_ref, fmr_ref, o_ref, n_ref = refs
    else:
        x_ref, pt_ref, ptr_ref, rm_ref, o_ref = refs
    wide_parts = x_ref.shape[0]
    row_at = lax.broadcasted_iota(jnp.int32, (FEEDS, FEEDS), 0)
    col_at = lax.broadcasted_iota(jnp.int32, (FEEDS, FEEDS), 1)
    upper = col_at >= row_at

    if with_counts:
        @pl.when(pl.program_id(0) == 0)
        def _():
            def write_count(slot, value):
                n_ref[pl.ds(slot, 1), :] = value

            diag_pairs(fm_ref[...], fmr_ref[...], upper, write_count)

    g = None
    gr = None
    for w in range(wide_parts):
        xw = x_ref[w].reshape(-1, x_ref.shape[-1])
        gw = lax.dot_general(pt_ref[w], xw, NT, preferred_element_type=jnp.float32)
        grw = lax.dot_general(ptr_ref[w], xw, NT, preferred_element_type=jnp.float32)
        g = gw if g is None else g + gw
        gr = grw if gr is None else gr + grw
    g = g.astype(jnp.bfloat16)
    gr = gr.astype(jnp.bfloat16)
    yr = jnp.dot(gr, rm_ref[...], preferred_element_type=jnp.float32).astype(jnp.bfloat16)
    for part, right in enumerate((gr, yr)):
        def write_vis(slot, value, part=part):
            o_ref[0, part, pl.ds(slot, 1), :] = value

        diag_pairs(g, right, upper, write_vis)


def correlate(blocks, pt, ptr, rm, fm=None, fmr=None):
    wide_parts, tm_parts, local_channels, rows_each, inputs_each = blocks.shape
    with_counts = fm is not None
    in_specs = [
        pl.BlockSpec((wide_parts, tm_parts, None, rows_each, inputs_each), lambda c: (0, 0, c, 0, 0)),
        pl.BlockSpec(pt.shape, lambda c: (0, 0, 0)),
        pl.BlockSpec(ptr.shape, lambda c: (0, 0, 0)),
        pl.BlockSpec(rm.shape, lambda c: (0, 0)),
    ]
    out_specs = [pl.BlockSpec((1, 2, CYL * CYL, FEEDS), lambda c: (c, 0, 0, 0))]
    out_shape = [jax.ShapeDtypeStruct((local_channels, 2, CYL * CYL, FEEDS), jnp.float32)]
    operands = [blocks, pt, ptr, rm]
    if with_counts:
        in_specs += [pl.BlockSpec(fm.shape, lambda c: (0, 0)), pl.BlockSpec(fmr.shape, lambda c: (0, 0))]
        out_specs.append(pl.BlockSpec((CYL * CYL, FEEDS), lambda c: (0, 0)))
        out_shape.append(jax.ShapeDtypeStruct((CYL * CYL, FEEDS), jnp.float32))
        operands += [fm, fmr]
    positions = CYL * FEEDS
    rows = tm_parts * rows_each
    flops = local_channels * (
        2 * 2 * positions * wide_parts * inputs_each * rows + 2 * positions * rows * rows
        + 20 * 2 * FEEDS * FEEDS * rows
    )
    bytes_accessed = blocks.size * 2 + pt.size * 4 + local_channels * 2 * CYL * CYL * FEEDS * 4
    return pl.pallas_call(
        functools.partial(correlate_kernel, with_counts=with_counts),
        grid=(local_channels,),
        in_specs=in_specs,
        out_specs=out_specs,
        out_shape=out_shape,
        cost_estimate=pl.CostEstimate(flops=flops, transcendentals=0, bytes_accessed=bytes_accessed),
    )(*operands)


def unskew(sums, sign):
    pieces = {}
    for a in range(CYL):
        for b in range(a, CYL):
            forward = jnp.flip(sums[..., a * CYL + b, :], axis=-1)
            pieces[(a, b)] = forward
            if a < b:
                lower = sums[..., b * CYL + a, :]
                backward = jnp.concatenate([forward[..., :1], lower[..., : FEEDS - 1]], axis=-1)
                pieces[(b, a)] = backward * sign
    stacked = jnp.stack([pieces[(a, b)] for a in range(CYL) for b in range(CYL)], axis=-2)
    return stacked * pair_keep().reshape(CYL * CYL, FEEDS)


def body(samples, feed_input_wiring, input_flags):
    frames_here, inputs_here, length = samples.shape
    tm_parts = lax.axis_size("tm")
    wide_parts = lax.axis_size("wide")
    devices = tm_parts * wide_parts
    frames_all = frames_here * tm_parts
    local_channels = CH // devices
    table = channel_table_const(NSAMP, CH, CHAN_LO)
    chunks = math.gcd(4, local_channels)
    chunk_channels = local_channels // chunks
    table = table.reshape(devices, chunks, chunk_channels * 2, length).transpose(1, 0, 2, 3)
    table = jnp.asarray(table.reshape(chunks, devices * chunk_channels * 2, length), dtype=jnp.bfloat16)
    flattened = samples.reshape(frames_here * inputs_here, length)
    chunk_rows = devices * chunk_channels * 2
    table = table.reshape(chunks * chunk_rows, length)

    def channelize(rows):
        spectra = lax.dot_general(rows, flattened, NT, preferred_element_type=jnp.float32)
        return spectra.astype(jnp.bfloat16).reshape(-1, devices, chunk_channels, 2 * frames_here, inputs_here)

    spectra = [channelize(table[:chunk_rows])[0]]
    if chunks > 1:
        rest = channelize(table[chunk_rows:])
        spectra += [rest[j] for j in range(chunks - 1)]

    inputs_all = wide_parts * inputs_here
    flags = input_flags.astype(jnp.bfloat16)
    source = jnp.arange(inputs_all, dtype=jnp.int32)
    wiring_rev = jnp.flip(feed_input_wiring.reshape(CYL, FEEDS), axis=1).reshape(CYL * FEEDS)
    pt_full = jnp.where(feed_input_wiring[:, None] == source[None, :], flags[None, :], jnp.bfloat16(0))
    ptr_full = jnp.where(wiring_rev[:, None] == source[None, :], flags[None, :], jnp.bfloat16(0))
    first_lane = (lax.broadcasted_iota(jnp.int32, (CYL * FEEDS, 128), 1) == 0).astype(jnp.bfloat16)
    fm = jnp.sum(pt_full.astype(jnp.float32), axis=1).astype(jnp.bfloat16)[:, None] * first_lane
    fmr = jnp.sum(ptr_full.astype(jnp.float32), axis=1).astype(jnp.bfloat16)[:, None] * first_lane
    pt = pt_full.reshape(CYL * FEEDS, wide_parts, inputs_here).transpose(1, 0, 2)
    ptr = ptr_full.reshape(CYL * FEEDS, wide_parts, inputs_here).transpose(1, 0, 2)

    rows = tm_parts * 2 * frames_here
    r_at = np.arange(rows)
    frame_at = r_at % frames_here
    part_at = (r_at // frames_here) % 2
    group_at = r_at // (2 * frames_here)
    rm = np.zeros((rows, rows), np.float32)
    for r in range(rows):
        partner = group_at[r] * 2 * frames_here + (1 - part_at[r]) * frames_here + frame_at[r]
        rm[partner, r] = -1.0 if part_at[r] == 0 else 1.0
    rm = jnp.asarray(rm, dtype=jnp.bfloat16)

    sums = []
    for j in range(chunks):
        spectra_j = spectra[j]
        if j >= 2:
            spectra_j, _ = lax.optimization_barrier((spectra_j, sums[j - 2]))
        turned = lax.all_to_all(spectra_j, ("wide", "tm"), 0, 0, tiled=True)
        blk = turned.reshape(wide_parts, tm_parts, chunk_channels, 2 * frames_here, inputs_here)
        if j == 0:
            first, count_sums = correlate(blk, pt, ptr, rm, fm, fmr)
            sums.append(first)
        else:
            sums.append(correlate(blk, pt, ptr, rm)[0])
    sums = jnp.concatenate(sums, axis=0)
    conj_sign = jnp.array([1.0, -1.0], jnp.float32)[None, :, None]
    vis = unskew(sums, conj_sign)
    local_baselines = NBASE // devices
    send = vis.reshape(local_channels, 2, devices, local_baselines).transpose(2, 0, 1, 3)
    received = lax.all_to_all(send, ("wide", "tm"), 0, 0, tiled=True)
    stacked_in = received.reshape(CH * 2, local_baselines)
    device_position = lax.axis_index("wide") * tm_parts + lax.axis_index("tm")
    global_stack_counts = unskew(count_sums, 1.0).reshape(NBASE)
    local_stack_counts = lax.dynamic_slice_in_dim(
        global_stack_counts, device_position * local_baselines, local_baselines
    )
    delay = delay_matrix_const(CH)
    spectra_out = lax.dot_general(
        stacked_in, delay, (((0,), (0,)), ((), ())), precision=lax.Precision.HIGH,
        preferred_element_type=jnp.float32,
    )
    weight = 1.0 / jnp.sqrt(frames_all * CH * jnp.maximum(local_stack_counts, 1.0))
    return spectra_out.reshape(local_baselines, 2, CH) * weight[:, None, None]


def solution(mesh):
    return jax.shard_map(
        body,
        mesh=mesh,
        in_specs=(P("tm", "wide", None), P(), P()),
        out_specs=P(("wide", "tm"), None, None),
        check_vma=False,
    )
```

```python
import functools
import math

import numpy as np
import jax
import jax.numpy as jnp
from jax import lax
from jax.experimental import pallas as pl
from jax.experimental.pallas import tpu as pltpu
from jax.sharding import PartitionSpec as P

CYL = 4
FEEDS = 256
NSAMP = 2048
CH = 512
CHAN_LO = 256
NBASE = 4096

NT = (((1,), (1,)), ((), ()))


def channel_table_const(length, frequency_channels, first):
    samples_at = np.arange(length, dtype=np.int64)
    channel_at = np.arange(frequency_channels, dtype=np.int64) + first
    turns = (channel_at[:, None] * samples_at[None, :]) % length
    phase = turns.astype(np.float32) * np.float32(2.0 * math.pi / length)
    scale = np.float32(1.0 / math.sqrt(length))
    both = np.stack([np.cos(phase) * scale, -np.sin(phase) * scale], axis=1)
    return both.reshape(2 * frequency_channels, length)


def delay_matrix_const(frequency_channels):
    index = np.arange(frequency_channels, dtype=np.int64)
    phase = ((index[:, None] * index[None, :]) % frequency_channels).astype(np.float32) * np.float32(
        2.0 * math.pi / frequency_channels
    )
    cosine = np.cos(phase).astype(np.float32)
    sine = np.sin(phase).astype(np.float32)
    w = np.zeros((frequency_channels, 2, 2, frequency_channels), np.float32)
    w[:, 0, 0] = cosine
    w[:, 1, 0] = sine
    w[:, 0, 1] = -sine
    w[:, 1, 1] = cosine
    return jnp.asarray(w.reshape(2 * frequency_channels, 2 * frequency_channels))


def pair_keep():
    same = jnp.eye(CYL, dtype=jnp.float32)[:, :, None]
    first = (jnp.arange(FEEDS, dtype=jnp.int32) == 0).astype(jnp.float32)[None, None, :]
    return 1.0 - same * first


def diag_pairs(left, right, upper, write):
    for a in range(CYL):
        for b in range(a, CYL):
            tile = lax.dot_general(
                left[a * FEEDS:(a + 1) * FEEDS], right[b * FEEDS:(b + 1) * FEEDS], NT,
                preferred_element_type=jnp.float32,
            )
            skewed = pltpu.roll(tile, 0, 1, stride=1, stride_axis=0)
            up = jnp.sum(jnp.where(upper, skewed, 0.0), axis=0, keepdims=True)
            write(a * CYL + b, up)
            if a < b:
                total = jnp.sum(skewed, axis=0, keepdims=True)
                write(b * CYL + a, total - up)


def correlate_kernel(*refs, with_counts):
    if with_counts:
        x_ref, pt_ref, j_ref, rm_ref, fm_ref, fmr_ref, o_ref, n_ref = refs
    else:
        x_ref, pt_ref, j_ref, rm_ref, o_ref = refs
    wide_parts = x_ref.shape[0]
    row_at = lax.broadcasted_iota(jnp.int32, (FEEDS, FEEDS), 0)
    col_at = lax.broadcasted_iota(jnp.int32, (FEEDS, FEEDS), 1)
    upper = col_at >= row_at

    if with_counts:
        @pl.when(pl.program_id(0) == 0)
        def _():
            def write_count(slot, value):
                n_ref[pl.ds(slot, 1), :] = value

            diag_pairs(fm_ref[...], fmr_ref[...], upper, write_count)

    g = None
    for w in range(wide_parts):
        xw = x_ref[w].reshape(-1, x_ref.shape[-1])
        gw = lax.dot_general(pt_ref[w], xw, NT, preferred_element_type=jnp.float32)
        g = gw if g is None else g + gw
    g = g.astype(jnp.bfloat16)
    flip = j_ref[...]
    gr = jnp.concatenate(
        [
            jnp.dot(flip, g[b * FEEDS:(b + 1) * FEEDS], preferred_element_type=jnp.float32)
            for b in range(CYL)
        ],
        axis=0,
    ).astype(jnp.bfloat16)
    yr = jnp.dot(gr, rm_ref[...], preferred_element_type=jnp.float32).astype(jnp.bfloat16)
    for part, right in enumerate((gr, yr)):
        def write_vis(slot, value, part=part):
            o_ref[0, part, pl.ds(slot, 1), :] = value

        diag_pairs(g, right, upper, write_vis)


def correlate(blocks, pt, flip, rm, fm=None, fmr=None):
    wide_parts, tm_parts, local_channels, rows_each, inputs_each = blocks.shape
    with_counts = fm is not None
    in_specs = [
        pl.BlockSpec((wide_parts, tm_parts, None, rows_each, inputs_each), lambda c: (0, 0, c, 0, 0)),
        pl.BlockSpec(pt.shape, lambda c: (0, 0, 0)),
        pl.BlockSpec(flip.shape, lambda c: (0, 0)),
        pl.BlockSpec(rm.shape, lambda c: (0, 0)),
    ]
    out_specs = [pl.BlockSpec((1, 2, CYL * CYL, FEEDS), lambda c: (c, 0, 0, 0))]
    out_shape = [jax.ShapeDtypeStruct((local_channels, 2, CYL * CYL, FEEDS), jnp.float32)]
    operands = [blocks, pt, flip, rm]
    if with_counts:
        in_specs += [pl.BlockSpec(fm.shape, lambda c: (0, 0)), pl.BlockSpec(fmr.shape, lambda c: (0, 0))]
        out_specs.append(pl.BlockSpec((CYL * CYL, FEEDS), lambda c: (0, 0)))
        out_shape.append(jax.ShapeDtypeStruct((CYL * CYL, FEEDS), jnp.float32))
        operands += [fm, fmr]
    positions = CYL * FEEDS
    rows = tm_parts * rows_each
    flops = local_channels * (
        2 * positions * wide_parts * inputs_each * rows + 2 * positions * FEEDS * rows
        + 2 * positions * rows * rows
        + 20 * 2 * FEEDS * FEEDS * rows
    )
    bytes_accessed = blocks.size * 2 + pt.size * 2 + local_channels * 2 * CYL * CYL * FEEDS * 4
    return pl.pallas_call(
        functools.partial(correlate_kernel, with_counts=with_counts),
        grid=(local_channels,),
        in_specs=in_specs,
        out_specs=out_specs,
        out_shape=out_shape,
        cost_estimate=pl.CostEstimate(flops=flops, transcendentals=0, bytes_accessed=bytes_accessed),
    )(*operands)


def unskew(sums, sign):
    pieces = {}
    for a in range(CYL):
        for b in range(a, CYL):
            forward = jnp.flip(sums[..., a * CYL + b, :], axis=-1)
            pieces[(a, b)] = forward
            if a < b:
                lower = sums[..., b * CYL + a, :]
                backward = jnp.concatenate([forward[..., :1], lower[..., : FEEDS - 1]], axis=-1)
                pieces[(b, a)] = backward * sign
    stacked = jnp.stack([pieces[(a, b)] for a in range(CYL) for b in range(CYL)], axis=-2)
    return stacked * pair_keep().reshape(CYL * CYL, FEEDS)


def body(samples, feed_input_wiring, input_flags):
    frames_here, inputs_here, length = samples.shape
    tm_parts = lax.axis_size("tm")
    wide_parts = lax.axis_size("wide")
    devices = tm_parts * wide_parts
    frames_all = frames_here * tm_parts
    local_channels = CH // devices
    table = channel_table_const(NSAMP, CH, CHAN_LO)
    chunks = math.gcd(4, local_channels)
    chunk_channels = local_channels // chunks
    table = table.reshape(devices, chunks, chunk_channels * 2, length).transpose(1, 0, 2, 3)
    table = jnp.asarray(table.reshape(chunks, devices * chunk_channels * 2, length), dtype=jnp.bfloat16)
    flattened = samples.reshape(frames_here * inputs_here, length)
    chunk_rows = devices * chunk_channels * 2
    table = table.reshape(chunks * chunk_rows, length)

    def channelize(rows):
        spectra = lax.dot_general(rows, flattened, NT, preferred_element_type=jnp.float32)
        return spectra.astype(jnp.bfloat16).reshape(-1, devices, chunk_channels, 2 * frames_here, inputs_here)

    spectra = [channelize(table[:chunk_rows])[0]]
    if chunks > 1:
        rest = channelize(table[chunk_rows:])
        spectra += [rest[j] for j in range(chunks - 1)]

    inputs_all = wide_parts * inputs_here
    flags = input_flags.astype(jnp.bfloat16)
    source = jnp.arange(inputs_all, dtype=jnp.int32)
    wiring_rev = jnp.flip(feed_input_wiring.reshape(CYL, FEEDS), axis=1).reshape(CYL * FEEDS)
    pt_full = jnp.where(feed_input_wiring[:, None] == source[None, :], flags[None, :], jnp.bfloat16(0))
    ptr_full = jnp.where(wiring_rev[:, None] == source[None, :], flags[None, :], jnp.bfloat16(0))
    first_lane = (lax.broadcasted_iota(jnp.int32, (CYL * FEEDS, 128), 1) == 0).astype(jnp.bfloat16)
    fm = jnp.sum(pt_full.astype(jnp.float32), axis=1).astype(jnp.bfloat16)[:, None] * first_lane
    fmr = jnp.sum(ptr_full.astype(jnp.float32), axis=1).astype(jnp.bfloat16)[:, None] * first_lane
    pt = pt_full.reshape(CYL * FEEDS, wide_parts, inputs_here).transpose(1, 0, 2)
    flip = jnp.asarray(np.eye(FEEDS, dtype=np.float32)[::-1], dtype=jnp.bfloat16)

    rows = tm_parts * 2 * frames_here
    r_at = np.arange(rows)
    frame_at = r_at % frames_here
    part_at = (r_at // frames_here) % 2
    group_at = r_at // (2 * frames_here)
    rm = np.zeros((rows, rows), np.float32)
    for r in range(rows):
        partner = group_at[r] * 2 * frames_here + (1 - part_at[r]) * frames_here + frame_at[r]
        rm[partner, r] = -1.0 if part_at[r] == 0 else 1.0
    rm = jnp.asarray(rm, dtype=jnp.bfloat16)

    sums = []
    for j in range(chunks):
        spectra_j = spectra[j]
        if j >= 2:
            spectra_j, _ = lax.optimization_barrier((spectra_j, sums[j - 2]))
        turned = lax.all_to_all(spectra_j, ("wide", "tm"), 0, 0, tiled=True)
        blk = turned.reshape(wide_parts, tm_parts, chunk_channels, 2 * frames_here, inputs_here)
        if j == 0:
            first, count_sums = correlate(blk, pt, flip, rm, fm, fmr)
            sums.append(first)
        else:
            sums.append(correlate(blk, pt, flip, rm)[0])
    sums = jnp.concatenate(sums, axis=0)
    conj_sign = jnp.array([1.0, -1.0], jnp.float32)[None, :, None]
    vis = unskew(sums, conj_sign)
    local_baselines = NBASE // devices
    send = vis.reshape(local_channels, 2, devices, local_baselines).transpose(2, 0, 1, 3)
    received = lax.all_to_all(send, ("wide", "tm"), 0, 0, tiled=True)
    stacked_in = received.reshape(CH * 2, local_baselines)
    device_position = lax.axis_index("wide") * tm_parts + lax.axis_index("tm")
    global_stack_counts = unskew(count_sums, 1.0).reshape(NBASE)
    local_stack_counts = lax.dynamic_slice_in_dim(
        global_stack_counts, device_position * local_baselines, local_baselines
    )
    delay = delay_matrix_const(CH)
    spectra_out = lax.dot_general(
        stacked_in, delay, (((0,), (0,)), ((), ())), precision=lax.Precision.HIGH,
        preferred_element_type=jnp.float32,
    )
    weight = 1.0 / jnp.sqrt(frames_all * CH * jnp.maximum(local_stack_counts, 1.0))
    return spectra_out.reshape(local_baselines, 2, CH) * weight[:, None, None]


def solution(mesh):
    return jax.shard_map(
        body,
        mesh=mesh,
        in_specs=(P("tm", "wide", None), P(), P()),
        out_specs=P(("wide", "tm"), None, None),
        check_vma=False,
    )
```

```python
import functools
import math

import numpy as np
import jax
import jax.numpy as jnp
from jax import lax
from jax.experimental import pallas as pl
from jax.experimental.pallas import tpu as pltpu
from jax.sharding import PartitionSpec as P

CYL = 4
FEEDS = 256
NSAMP = 2048
CH = 512
CHAN_LO = 256
NBASE = 4096

NT = (((1,), (1,)), ((), ()))


def channel_table_const(length, frequency_channels, first):
    samples_at = np.arange(length, dtype=np.int64)
    channel_at = np.arange(frequency_channels, dtype=np.int64) + first
    turns = (channel_at[:, None] * samples_at[None, :]) % length
    phase = turns.astype(np.float32) * np.float32(2.0 * math.pi / length)
    scale = np.float32(1.0 / math.sqrt(length))
    both = np.stack([np.cos(phase) * scale, -np.sin(phase) * scale], axis=1)
    return both.reshape(2 * frequency_channels, length)


def delay_matrix_const(frequency_channels):
    index = np.arange(frequency_channels, dtype=np.int64)
    phase = ((index[:, None] * index[None, :]) % frequency_channels).astype(np.float32) * np.float32(
        2.0 * math.pi / frequency_channels
    )
    cosine = np.cos(phase).astype(np.float32)
    sine = np.sin(phase).astype(np.float32)
    w = np.zeros((frequency_channels, 2, 2, frequency_channels), np.float32)
    w[:, 0, 0] = cosine
    w[:, 1, 0] = sine
    w[:, 0, 1] = -sine
    w[:, 1, 1] = cosine
    return jnp.asarray(w.reshape(2 * frequency_channels, 2 * frequency_channels))


def pair_keep():
    same = jnp.eye(CYL, dtype=jnp.float32)[:, :, None]
    first = (jnp.arange(FEEDS, dtype=jnp.int32) == 0).astype(jnp.float32)[None, None, :]
    return 1.0 - same * first


def diag_pairs(left, right, upper, write):
    for a in range(CYL):
        for b in range(a, CYL):
            tile = lax.dot_general(
                left[a * FEEDS:(a + 1) * FEEDS], right[b * FEEDS:(b + 1) * FEEDS], NT,
                preferred_element_type=jnp.float32,
            )
            skewed = pltpu.roll(tile, 0, 1, stride=1, stride_axis=0)
            up = jnp.sum(jnp.where(upper, skewed, 0.0), axis=0, keepdims=True)
            write(a * CYL + b, up)
            if a < b:
                total = jnp.sum(skewed, axis=0, keepdims=True)
                write(b * CYL + a, total - up)


def correlate_kernel(*refs, with_counts):
    if with_counts:
        x_ref, pt_ref, ptr_ref, rm_ref, fm_ref, fmr_ref, o_ref, n_ref = refs
    else:
        x_ref, pt_ref, ptr_ref, rm_ref, o_ref = refs
    wide_parts = x_ref.shape[0]
    row_at = lax.broadcasted_iota(jnp.int32, (FEEDS, FEEDS), 0)
    col_at = lax.broadcasted_iota(jnp.int32, (FEEDS, FEEDS), 1)
    upper = col_at >= row_at

    if with_counts:
        @pl.when(pl.program_id(0) == 0)
        def _():
            def write_count(slot, value):
                n_ref[pl.ds(slot, 1), :] = value

            diag_pairs(fm_ref[...], fmr_ref[...], upper, write_count)

    g = None
    gr = None
    for w in range(wide_parts):
        xw = x_ref[w].reshape(-1, x_ref.shape[-1])
        gw = lax.dot_general(pt_ref[w], xw, NT, preferred_element_type=jnp.float32)
        grw = lax.dot_general(ptr_ref[w], xw, NT, preferred_element_type=jnp.float32)
        g = gw if g is None else g + gw
        gr = grw if gr is None else gr + grw
    g = g.astype(jnp.bfloat16)
    gr = gr.astype(jnp.bfloat16)
    yr = jnp.dot(gr, rm_ref[...], preferred_element_type=jnp.float32).astype(jnp.bfloat16)
    for part, right in enumerate((gr, yr)):
        def write_vis(slot, value, part=part):
            o_ref[0, part, pl.ds(slot, 1), :] = value

        diag_pairs(g, right, upper, write_vis)


def correlate(blocks, pt, ptr, rm, fm=None, fmr=None):
    wide_parts, tm_parts, local_channels, rows_each, inputs_each = blocks.shape
    with_counts = fm is not None
    in_specs = [
        pl.BlockSpec((wide_parts, tm_parts, None, rows_each, inputs_each), lambda c: (0, 0, c, 0, 0)),
        pl.BlockSpec(pt.shape, lambda c: (0, 0, 0)),
        pl.BlockSpec(ptr.shape, lambda c: (0, 0, 0)),
        pl.BlockSpec(rm.shape, lambda c: (0, 0)),
    ]
    out_specs = [pl.BlockSpec((1, 2, CYL * CYL, FEEDS), lambda c: (c, 0, 0, 0))]
    out_shape = [jax.ShapeDtypeStruct((local_channels, 2, CYL * CYL, FEEDS), jnp.float32)]
    operands = [blocks, pt, ptr, rm]
    if with_counts:
        in_specs += [pl.BlockSpec(fm.shape, lambda c: (0, 0)), pl.BlockSpec(fmr.shape, lambda c: (0, 0))]
        out_specs.append(pl.BlockSpec((CYL * CYL, FEEDS), lambda c: (0, 0)))
        out_shape.append(jax.ShapeDtypeStruct((CYL * CYL, FEEDS), jnp.float32))
        operands += [fm, fmr]
    positions = CYL * FEEDS
    rows = tm_parts * rows_each
    flops = local_channels * (
        2 * 2 * positions * wide_parts * inputs_each * rows + 2 * positions * rows * rows
        + 20 * 2 * FEEDS * FEEDS * rows
    )
    bytes_accessed = blocks.size * 2 + pt.size * 4 + local_channels * 2 * CYL * CYL * FEEDS * 4
    return pl.pallas_call(
        functools.partial(correlate_kernel, with_counts=with_counts),
        grid=(local_channels,),
        in_specs=in_specs,
        out_specs=out_specs,
        out_shape=out_shape,
        cost_estimate=pl.CostEstimate(flops=flops, transcendentals=0, bytes_accessed=bytes_accessed),
    )(*operands)


def unskew(sums, sign):
    pieces = {}
    for a in range(CYL):
        for b in range(a, CYL):
            forward = jnp.flip(sums[..., a * CYL + b, :], axis=-1)
            pieces[(a, b)] = forward
            if a < b:
                lower = sums[..., b * CYL + a, :]
                backward = jnp.concatenate([forward[..., :1], lower[..., : FEEDS - 1]], axis=-1)
                pieces[(b, a)] = backward * sign
    stacked = jnp.stack([pieces[(a, b)] for a in range(CYL) for b in range(CYL)], axis=-2)
    return stacked * pair_keep().reshape(CYL * CYL, FEEDS)


def body(samples, feed_input_wiring, input_flags):
    frames_here, inputs_here, length = samples.shape
    tm_parts = lax.axis_size("tm")
    wide_parts = lax.axis_size("wide")
    devices = tm_parts * wide_parts
    frames_all = frames_here * tm_parts
    local_channels = CH // devices
    table = channel_table_const(NSAMP, CH, CHAN_LO)
    chunks = math.gcd(2, local_channels)
    chunk_channels = local_channels // chunks
    table = table.reshape(devices, chunks, chunk_channels * 2, length).transpose(1, 0, 2, 3)
    table = jnp.asarray(table.reshape(chunks, devices * chunk_channels * 2, length), dtype=jnp.bfloat16)
    flattened = samples.reshape(frames_here * inputs_here, length)
    chunk_rows = devices * chunk_channels * 2
    table = table.reshape(chunks * chunk_rows, length)

    def channelize(rows):
        spectra = lax.dot_general(rows, flattened, NT, preferred_element_type=jnp.float32)
        return spectra.astype(jnp.bfloat16).reshape(-1, devices, chunk_channels, 2 * frames_here, inputs_here)

    spectra = [channelize(table[:chunk_rows])[0]]
    if chunks > 1:
        rest = channelize(table[chunk_rows:])
        spectra += [rest[j] for j in range(chunks - 1)]

    inputs_all = wide_parts * inputs_here
    flags = input_flags.astype(jnp.bfloat16)
    source = jnp.arange(inputs_all, dtype=jnp.int32)
    wiring_rev = jnp.flip(feed_input_wiring.reshape(CYL, FEEDS), axis=1).reshape(CYL * FEEDS)
    pt_full = jnp.where(feed_input_wiring[:, None] == source[None, :], flags[None, :], jnp.bfloat16(0))
    ptr_full = jnp.where(wiring_rev[:, None] == source[None, :], flags[None, :], jnp.bfloat16(0))
    first_lane = (lax.broadcasted_iota(jnp.int32, (CYL * FEEDS, 128), 1) == 0).astype(jnp.bfloat16)
    fm = jnp.sum(pt_full.astype(jnp.float32), axis=1).astype(jnp.bfloat16)[:, None] * first_lane
    fmr = jnp.sum(ptr_full.astype(jnp.float32), axis=1).astype(jnp.bfloat16)[:, None] * first_lane
    pt = pt_full.reshape(CYL * FEEDS, wide_parts, inputs_here).transpose(1, 0, 2)
    ptr = ptr_full.reshape(CYL * FEEDS, wide_parts, inputs_here).transpose(1, 0, 2)

    rows = tm_parts * 2 * frames_here
    r_at = np.arange(rows)
    frame_at = r_at % frames_here
    part_at = (r_at // frames_here) % 2
    group_at = r_at // (2 * frames_here)
    rm = np.zeros((rows, rows), np.float32)
    for r in range(rows):
        partner = group_at[r] * 2 * frames_here + (1 - part_at[r]) * frames_here + frame_at[r]
        rm[partner, r] = -1.0 if part_at[r] == 0 else 1.0
    rm = jnp.asarray(rm, dtype=jnp.bfloat16)

    sums = []
    for j in range(chunks):
        spectra_j = spectra[j]
        if j >= 2:
            spectra_j, _ = lax.optimization_barrier((spectra_j, sums[j - 2]))
        turned = lax.all_to_all(spectra_j, ("wide", "tm"), 0, 0, tiled=True)
        blk = turned.reshape(wide_parts, tm_parts, chunk_channels, 2 * frames_here, inputs_here)
        if j == 0:
            first, count_sums = correlate(blk, pt, ptr, rm, fm, fmr)
            sums.append(first)
        else:
            sums.append(correlate(blk, pt, ptr, rm)[0])
    sums = jnp.concatenate(sums, axis=0)
    conj_sign = jnp.array([1.0, -1.0], jnp.float32)[None, :, None]
    vis = unskew(sums, conj_sign)
    local_baselines = NBASE // devices
    send = vis.reshape(local_channels, 2, devices, local_baselines).transpose(2, 0, 1, 3)
    received = lax.all_to_all(send, ("wide", "tm"), 0, 0, tiled=True)
    stacked_in = received.reshape(CH * 2, local_baselines)
    device_position = lax.axis_index("wide") * tm_parts + lax.axis_index("tm")
    global_stack_counts = unskew(count_sums, 1.0).reshape(NBASE)
    local_stack_counts = lax.dynamic_slice_in_dim(
        global_stack_counts, device_position * local_baselines, local_baselines
    )
    delay = delay_matrix_const(CH)
    spectra_out = lax.dot_general(
        stacked_in, delay, (((0,), (0,)), ((), ())), precision=lax.Precision.HIGH,
        preferred_element_type=jnp.float32,
    )
    weight = 1.0 / jnp.sqrt(frames_all * CH * jnp.maximum(local_stack_counts, 1.0))
    return spectra_out.reshape(local_baselines, 2, CH) * weight[:, None, None]


def solution(mesh):
    return jax.shard_map(
        body,
        mesh=mesh,
        in_specs=(P("tm", "wide", None), P(), P()),
        out_specs=P(("wide", "tm"), None, None),
        check_vma=False,
    )
```

```python
import functools
import math

import numpy as np
import jax
import jax.numpy as jnp
from jax import lax
from jax.experimental import pallas as pl
from jax.experimental.pallas import tpu as pltpu
from jax.sharding import PartitionSpec as P

CYL = 4
FEEDS = 256
NSAMP = 2048
CH = 512
CHAN_LO = 256
NBASE = 4096

NT = (((1,), (1,)), ((), ()))


def channel_table_const(length, frequency_channels, first):
    samples_at = np.arange(length, dtype=np.int64)
    channel_at = np.arange(frequency_channels, dtype=np.int64) + first
    turns = (channel_at[:, None] * samples_at[None, :]) % length
    phase = turns.astype(np.float32) * np.float32(2.0 * math.pi / length)
    scale = np.float32(1.0 / math.sqrt(length))
    both = np.stack([np.cos(phase) * scale, -np.sin(phase) * scale], axis=1)
    return both.reshape(2 * frequency_channels, length)


def delay_matrix_const(frequency_channels):
    index = np.arange(frequency_channels, dtype=np.int64)
    phase = ((index[:, None] * index[None, :]) % frequency_channels).astype(np.float32) * np.float32(
        2.0 * math.pi / frequency_channels
    )
    cosine = np.cos(phase).astype(np.float32)
    sine = np.sin(phase).astype(np.float32)
    w = np.zeros((frequency_channels, 2, 2, frequency_channels), np.float32)
    w[:, 0, 0] = cosine
    w[:, 1, 0] = sine
    w[:, 0, 1] = -sine
    w[:, 1, 1] = cosine
    return jnp.asarray(w.reshape(2 * frequency_channels, 2 * frequency_channels))


def pair_keep():
    same = jnp.eye(CYL, dtype=jnp.float32)[:, :, None]
    first = (jnp.arange(FEEDS, dtype=jnp.int32) == 0).astype(jnp.float32)[None, None, :]
    return 1.0 - same * first


def diag_pairs(left, right, upper, write):
    for a in range(CYL):
        for b in range(a, CYL):
            tile = lax.dot_general(
                left[a * FEEDS:(a + 1) * FEEDS], right[b * FEEDS:(b + 1) * FEEDS], NT,
                preferred_element_type=jnp.float32,
            )
            skewed = pltpu.roll(tile, 0, 1, stride=1, stride_axis=0)
            up = jnp.sum(jnp.where(upper, skewed, 0.0), axis=0, keepdims=True)
            write(a * CYL + b, up)
            if a < b:
                total = jnp.sum(skewed, axis=0, keepdims=True)
                write(b * CYL + a, total - up)


def correlate_kernel(*refs, with_counts):
    if with_counts:
        x_ref, pt_ref, ptr_ref, rm_ref, fm_ref, fmr_ref, o_ref, n_ref = refs
    else:
        x_ref, pt_ref, ptr_ref, rm_ref, o_ref = refs
    wide_parts = x_ref.shape[0]
    row_at = lax.broadcasted_iota(jnp.int32, (FEEDS, FEEDS), 0)
    col_at = lax.broadcasted_iota(jnp.int32, (FEEDS, FEEDS), 1)
    upper = col_at >= row_at

    if with_counts:
        @pl.when(pl.program_id(0) == 0)
        def _():
            def write_count(slot, value):
                n_ref[pl.ds(slot, 1), :] = value

            diag_pairs(fm_ref[...], fmr_ref[...], upper, write_count)

    g = None
    gr = None
    for w in range(wide_parts):
        xw = x_ref[w].reshape(-1, x_ref.shape[-1])
        gw = lax.dot_general(pt_ref[w], xw, NT, preferred_element_type=jnp.float32)
        grw = lax.dot_general(ptr_ref[w], xw, NT, preferred_element_type=jnp.float32)
        g = gw if g is None else g + gw
        gr = grw if gr is None else gr + grw
    g = g.astype(jnp.bfloat16)
    gr = gr.astype(jnp.bfloat16)
    yr = jnp.dot(gr, rm_ref[...], preferred_element_type=jnp.float32).astype(jnp.bfloat16)
    for part, right in enumerate((gr, yr)):
        def write_vis(slot, value, part=part):
            o_ref[0, part, pl.ds(slot, 1), :] = value

        diag_pairs(g, right, upper, write_vis)


def correlate(blocks, pt, ptr, rm, fm=None, fmr=None):
    wide_parts, tm_parts, local_channels, rows_each, inputs_each = blocks.shape
    with_counts = fm is not None
    in_specs = [
        pl.BlockSpec((wide_parts, tm_parts, None, rows_each, inputs_each), lambda c: (0, 0, c, 0, 0)),
        pl.BlockSpec(pt.shape, lambda c: (0, 0, 0)),
        pl.BlockSpec(ptr.shape, lambda c: (0, 0, 0)),
        pl.BlockSpec(rm.shape, lambda c: (0, 0)),
    ]
    out_specs = [pl.BlockSpec((1, 2, CYL * CYL, FEEDS), lambda c: (c, 0, 0, 0))]
    out_shape = [jax.ShapeDtypeStruct((local_channels, 2, CYL * CYL, FEEDS), jnp.float32)]
    operands = [blocks, pt, ptr, rm]
    if with_counts:
        in_specs += [pl.BlockSpec(fm.shape, lambda c: (0, 0)), pl.BlockSpec(fmr.shape, lambda c: (0, 0))]
        out_specs.append(pl.BlockSpec((CYL * CYL, FEEDS), lambda c: (0, 0)))
        out_shape.append(jax.ShapeDtypeStruct((CYL * CYL, FEEDS), jnp.float32))
        operands += [fm, fmr]
    positions = CYL * FEEDS
    rows = tm_parts * rows_each
    flops = local_channels * (
        2 * 2 * positions * wide_parts * inputs_each * rows + 2 * positions * rows * rows
        + 20 * 2 * FEEDS * FEEDS * rows
    )
    bytes_accessed = blocks.size * 2 + pt.size * 4 + local_channels * 2 * CYL * CYL * FEEDS * 4
    return pl.pallas_call(
        functools.partial(correlate_kernel, with_counts=with_counts),
        grid=(local_channels,),
        in_specs=in_specs,
        out_specs=out_specs,
        out_shape=out_shape,
        cost_estimate=pl.CostEstimate(flops=flops, transcendentals=0, bytes_accessed=bytes_accessed),
    )(*operands)


def unskew(sums, sign):
    pieces = {}
    for a in range(CYL):
        for b in range(a, CYL):
            forward = jnp.flip(sums[..., a * CYL + b, :], axis=-1)
            pieces[(a, b)] = forward
            if a < b:
                lower = sums[..., b * CYL + a, :]
                backward = jnp.concatenate([forward[..., :1], lower[..., : FEEDS - 1]], axis=-1)
                pieces[(b, a)] = backward * sign
    stacked = jnp.stack([pieces[(a, b)] for a in range(CYL) for b in range(CYL)], axis=-2)
    return stacked * pair_keep().reshape(CYL * CYL, FEEDS)


def body(samples, feed_input_wiring, input_flags):
    frames_here, inputs_here, length = samples.shape
    tm_parts = lax.axis_size("tm")
    wide_parts = lax.axis_size("wide")
    devices = tm_parts * wide_parts
    frames_all = frames_here * tm_parts
    local_channels = CH // devices
    table = channel_table_const(NSAMP, CH, CHAN_LO)
    chunks = math.gcd(2, local_channels)
    chunk_channels = local_channels // chunks
    table = table.reshape(devices, chunks, chunk_channels * 2, length).transpose(1, 0, 2, 3)
    table = jnp.asarray(table.reshape(chunks, devices * chunk_channels * 2, length), dtype=jnp.bfloat16)
    flattened = samples.reshape(frames_here * inputs_here, length)
    chunk_rows = devices * chunk_channels * 2
    table = table.reshape(chunks * chunk_rows, length)

    def channelize(rows):
        spectra = lax.dot_general(rows, flattened, NT, preferred_element_type=jnp.float32)
        return spectra.astype(jnp.bfloat16).reshape(-1, devices, chunk_channels, 2 * frames_here, inputs_here)

    spectra = [channelize(table[:chunk_rows])[0]]
    if chunks > 1:
        rest = channelize(table[chunk_rows:])
        spectra += [rest[j] for j in range(chunks - 1)]

    inputs_all = wide_parts * inputs_here
    flags = input_flags.astype(jnp.bfloat16)
    source = jnp.arange(inputs_all, dtype=jnp.int32)
    wiring_rev = jnp.flip(feed_input_wiring.reshape(CYL, FEEDS), axis=1).reshape(CYL * FEEDS)
    pt_full = jnp.where(feed_input_wiring[:, None] == source[None, :], flags[None, :], jnp.bfloat16(0))
    ptr_full = jnp.where(wiring_rev[:, None] == source[None, :], flags[None, :], jnp.bfloat16(0))
    first_lane = (lax.broadcasted_iota(jnp.int32, (CYL * FEEDS, 128), 1) == 0).astype(jnp.bfloat16)
    fm = jnp.sum(pt_full.astype(jnp.float32), axis=1).astype(jnp.bfloat16)[:, None] * first_lane
    fmr = jnp.sum(ptr_full.astype(jnp.float32), axis=1).astype(jnp.bfloat16)[:, None] * first_lane
    pt = pt_full.reshape(CYL * FEEDS, wide_parts, inputs_here).transpose(1, 0, 2)
    ptr = ptr_full.reshape(CYL * FEEDS, wide_parts, inputs_here).transpose(1, 0, 2)

    rows = tm_parts * 2 * frames_here
    r_at = np.arange(rows)
    frame_at = r_at % frames_here
    part_at = (r_at // frames_here) % 2
    group_at = r_at // (2 * frames_here)
    rm = np.zeros((rows, rows), np.float32)
    for r in range(rows):
        partner = group_at[r] * 2 * frames_here + (1 - part_at[r]) * frames_here + frame_at[r]
        rm[partner, r] = -1.0 if part_at[r] == 0 else 1.0
    rm = jnp.asarray(rm, dtype=jnp.bfloat16)

    sums = []
    for j in range(chunks):
        spectra_j = spectra[j]
        if j >= 2:
            spectra_j, _ = lax.optimization_barrier((spectra_j, sums[j - 2]))
        elif j == 1:
            spectra_j, pt, ptr, fm, fmr = lax.optimization_barrier((spectra_j, pt, ptr, fm, fmr))
        turned = lax.all_to_all(spectra_j, ("wide", "tm"), 0, 0, tiled=True)
        blk = turned.reshape(wide_parts, tm_parts, chunk_channels, 2 * frames_here, inputs_here)
        if j == 0:
            first, count_sums = correlate(blk, pt, ptr, rm, fm, fmr)
            sums.append(first)
        else:
            sums.append(correlate(blk, pt, ptr, rm)[0])
    sums = jnp.concatenate(sums, axis=0)
    conj_sign = jnp.array([1.0, -1.0], jnp.float32)[None, :, None]
    vis = unskew(sums, conj_sign)
    local_baselines = NBASE // devices
    send = vis.reshape(local_channels, 2, devices, local_baselines).transpose(2, 0, 1, 3)
    received = lax.all_to_all(send, ("wide", "tm"), 0, 0, tiled=True)
    stacked_in = received.reshape(CH * 2, local_baselines)
    device_position = lax.axis_index("wide") * tm_parts + lax.axis_index("tm")
    global_stack_counts = unskew(count_sums, 1.0).reshape(NBASE)
    local_stack_counts = lax.dynamic_slice_in_dim(
        global_stack_counts, device_position * local_baselines, local_baselines
    )
    delay = delay_matrix_const(CH)
    spectra_out = lax.dot_general(
        stacked_in, delay, (((0,), (0,)), ((), ())), precision=lax.Precision.HIGH,
        preferred_element_type=jnp.float32,
    )
    weight = 1.0 / jnp.sqrt(frames_all * CH * jnp.maximum(local_stack_counts, 1.0))
    return spectra_out.reshape(local_baselines, 2, CH) * weight[:, None, None]


def solution(mesh):
    return jax.shard_map(
        body,
        mesh=mesh,
        in_specs=(P("tm", "wide", None), P(), P()),
        out_specs=P(("wide", "tm"), None, None),
        check_vma=False,
    )
```

```python
import functools
import math

import numpy as np
import jax
import jax.numpy as jnp
from jax import lax
from jax.experimental import pallas as pl
from jax.experimental.pallas import tpu as pltpu
from jax.sharding import PartitionSpec as P

CYL = 4
FEEDS = 256
NSAMP = 2048
CH = 512
CHAN_LO = 256
NBASE = 4096

NT = (((1,), (1,)), ((), ()))


def channel_table_const(length, frequency_channels, first):
    samples_at = np.arange(length, dtype=np.int64)
    channel_at = np.arange(frequency_channels, dtype=np.int64) + first
    turns = (channel_at[:, None] * samples_at[None, :]) % length
    phase = turns.astype(np.float32) * np.float32(2.0 * math.pi / length)
    scale = np.float32(1.0 / math.sqrt(length))
    both = np.stack([np.cos(phase) * scale, -np.sin(phase) * scale], axis=1)
    return both.reshape(2 * frequency_channels, length)


def delay_matrix_const(frequency_channels):
    index = np.arange(frequency_channels, dtype=np.int64)
    phase = ((index[:, None] * index[None, :]) % frequency_channels).astype(np.float32) * np.float32(
        2.0 * math.pi / frequency_channels
    )
    cosine = np.cos(phase).astype(np.float32)
    sine = np.sin(phase).astype(np.float32)
    w = np.zeros((frequency_channels, 2, 2, frequency_channels), np.float32)
    w[:, 0, 0] = cosine
    w[:, 1, 0] = sine
    w[:, 0, 1] = -sine
    w[:, 1, 1] = cosine
    return jnp.asarray(w.reshape(2 * frequency_channels, 2 * frequency_channels))


def pair_keep():
    same = jnp.eye(CYL, dtype=jnp.float32)[:, :, None]
    first = (jnp.arange(FEEDS, dtype=jnp.int32) == 0).astype(jnp.float32)[None, None, :]
    return 1.0 - same * first


def diag_pairs(left, right, upper, write):
    for a in range(CYL):
        for b in range(a, CYL):
            tile = lax.dot_general(
                left[a * FEEDS:(a + 1) * FEEDS], right[b * FEEDS:(b + 1) * FEEDS], NT,
                preferred_element_type=jnp.float32,
            )
            skewed = pltpu.roll(tile, 0, 1, stride=1, stride_axis=0)
            up = jnp.sum(jnp.where(upper, skewed, 0.0), axis=0, keepdims=True)
            write(a * CYL + b, up)
            if a < b:
                total = jnp.sum(skewed, axis=0, keepdims=True)
                write(b * CYL + a, total - up)


def correlate_kernel(*refs, with_counts):
    if with_counts:
        x_ref, pt_ref, ptr_ref, rm_ref, fm_ref, fmr_ref, o_ref, n_ref = refs
    else:
        x_ref, pt_ref, ptr_ref, rm_ref, o_ref = refs
    wide_parts = x_ref.shape[0]
    row_at = lax.broadcasted_iota(jnp.int32, (FEEDS, FEEDS), 0)
    col_at = lax.broadcasted_iota(jnp.int32, (FEEDS, FEEDS), 1)
    upper = col_at >= row_at

    if with_counts:
        @pl.when(pl.program_id(0) == 0)
        def _():
            def write_count(slot, value):
                n_ref[pl.ds(slot, 1), :] = value

            diag_pairs(fm_ref[...], fmr_ref[...], upper, write_count)

    g = None
    gr = None
    for w in range(wide_parts):
        xw = x_ref[w].reshape(-1, x_ref.shape[-1])
        gw = lax.dot_general(pt_ref[w], xw, NT, preferred_element_type=jnp.float32)
        grw = lax.dot_general(ptr_ref[w], xw, NT, preferred_element_type=jnp.float32)
        g = gw if g is None else g + gw
        gr = grw if gr is None else gr + grw
    g = g.astype(jnp.bfloat16)
    gr = gr.astype(jnp.bfloat16)
    yr = jnp.dot(gr, rm_ref[...], preferred_element_type=jnp.float32).astype(jnp.bfloat16)
    for part, right in enumerate((gr, yr)):
        def write_vis(slot, value, part=part):
            o_ref[0, part, pl.ds(slot, 1), :] = value

        diag_pairs(g, right, upper, write_vis)


def correlate(blocks, pt, ptr, rm, fm=None, fmr=None):
    wide_parts, tm_parts, local_channels, rows_each, inputs_each = blocks.shape
    with_counts = fm is not None
    in_specs = [
        pl.BlockSpec((wide_parts, tm_parts, None, rows_each, inputs_each), lambda c: (0, 0, c, 0, 0)),
        pl.BlockSpec(pt.shape, lambda c: (0, 0, 0)),
        pl.BlockSpec(ptr.shape, lambda c: (0, 0, 0)),
        pl.BlockSpec(rm.shape, lambda c: (0, 0)),
    ]
    out_specs = [pl.BlockSpec((1, 2, CYL * CYL, FEEDS), lambda c: (c, 0, 0, 0))]
    out_shape = [jax.ShapeDtypeStruct((local_channels, 2, CYL * CYL, FEEDS), jnp.float32)]
    operands = [blocks, pt, ptr, rm]
    if with_counts:
        in_specs += [pl.BlockSpec(fm.shape, lambda c: (0, 0)), pl.BlockSpec(fmr.shape, lambda c: (0, 0))]
        out_specs.append(pl.BlockSpec((CYL * CYL, FEEDS), lambda c: (0, 0)))
        out_shape.append(jax.ShapeDtypeStruct((CYL * CYL, FEEDS), jnp.float32))
        operands += [fm, fmr]
    positions = CYL * FEEDS
    rows = tm_parts * rows_each
    flops = local_channels * (
        2 * 2 * positions * wide_parts * inputs_each * rows + 2 * positions * rows * rows
        + 20 * 2 * FEEDS * FEEDS * rows
    )
    bytes_accessed = blocks.size * 2 + pt.size * 4 + local_channels * 2 * CYL * CYL * FEEDS * 4
    return pl.pallas_call(
        functools.partial(correlate_kernel, with_counts=with_counts),
        grid=(local_channels,),
        in_specs=in_specs,
        out_specs=out_specs,
        out_shape=out_shape,
        cost_estimate=pl.CostEstimate(flops=flops, transcendentals=0, bytes_accessed=bytes_accessed),
    )(*operands)


def unskew(sums, sign):
    lead = sums.shape[:-2]
    grid = sums.reshape(lead + (CYL, CYL, FEEDS))
    forward = jnp.flip(grid, axis=-1)
    shifted = jnp.roll(grid, 1, axis=-1)
    first_of_pair = jnp.swapaxes(forward, -3, -2)[..., :1]
    k_at = lax.broadcasted_iota(jnp.int32, (CYL, CYL, FEEDS), 2)
    a_at = lax.broadcasted_iota(jnp.int32, (CYL, CYL, FEEDS), 0)
    b_at = lax.broadcasted_iota(jnp.int32, (CYL, CYL, FEEDS), 1)
    backward = jnp.where(k_at == 0, first_of_pair, shifted) * sign
    joined = jnp.where(a_at <= b_at, forward, backward) * pair_keep()
    return joined.reshape(lead + (CYL * CYL, FEEDS))


def body(samples, feed_input_wiring, input_flags):
    frames_here, inputs_here, length = samples.shape
    tm_parts = lax.axis_size("tm")
    wide_parts = lax.axis_size("wide")
    devices = tm_parts * wide_parts
    frames_all = frames_here * tm_parts
    local_channels = CH // devices
    table = channel_table_const(NSAMP, CH, CHAN_LO)
    chunks = math.gcd(2, local_channels)
    chunk_channels = local_channels // chunks
    table = table.reshape(devices, chunks, chunk_channels * 2, length).transpose(1, 0, 2, 3)
    table = jnp.asarray(table.reshape(chunks, devices * chunk_channels * 2, length), dtype=jnp.bfloat16)
    flattened = samples.reshape(frames_here * inputs_here, length)
    chunk_rows = devices * chunk_channels * 2
    table = table.reshape(chunks * chunk_rows, length)

    def channelize(rows):
        spectra = lax.dot_general(rows, flattened, NT, preferred_element_type=jnp.float32)
        return spectra.astype(jnp.bfloat16).reshape(-1, devices, chunk_channels, 2 * frames_here, inputs_here)

    spectra = [channelize(table[:chunk_rows])[0]]
    if chunks > 1:
        rest = channelize(table[chunk_rows:])
        spectra += [rest[j] for j in range(chunks - 1)]

    inputs_all = wide_parts * inputs_here
    flags = input_flags.astype(jnp.bfloat16)
    source = jnp.arange(inputs_all, dtype=jnp.int32)
    wiring_rev = jnp.flip(feed_input_wiring.reshape(CYL, FEEDS), axis=1).reshape(CYL * FEEDS)
    pt_full = jnp.where(feed_input_wiring[:, None] == source[None, :], flags[None, :], jnp.bfloat16(0))
    ptr_full = jnp.where(wiring_rev[:, None] == source[None, :], flags[None, :], jnp.bfloat16(0))
    first_lane = (lax.broadcasted_iota(jnp.int32, (CYL * FEEDS, 128), 1) == 0).astype(jnp.bfloat16)
    fm = jnp.sum(pt_full.astype(jnp.float32), axis=1).astype(jnp.bfloat16)[:, None] * first_lane
    fmr = jnp.sum(ptr_full.astype(jnp.float32), axis=1).astype(jnp.bfloat16)[:, None] * first_lane
    pt = pt_full.reshape(CYL * FEEDS, wide_parts, inputs_here).transpose(1, 0, 2)
    ptr = ptr_full.reshape(CYL * FEEDS, wide_parts, inputs_here).transpose(1, 0, 2)

    rows = tm_parts * 2 * frames_here
    r_at = np.arange(rows)
    frame_at = r_at % frames_here
    part_at = (r_at // frames_here) % 2
    group_at = r_at // (2 * frames_here)
    rm = np.zeros((rows, rows), np.float32)
    for r in range(rows):
        partner = group_at[r] * 2 * frames_here + (1 - part_at[r]) * frames_here + frame_at[r]
        rm[partner, r] = -1.0 if part_at[r] == 0 else 1.0
    rm = jnp.asarray(rm, dtype=jnp.bfloat16)

    sums = []
    for j in range(chunks):
        spectra_j = spectra[j]
        if j >= 2:
            spectra_j, _ = lax.optimization_barrier((spectra_j, sums[j - 2]))
        elif j == 1:
            spectra_j, pt, ptr, fm, fmr = lax.optimization_barrier((spectra_j, pt, ptr, fm, fmr))
        turned = lax.all_to_all(spectra_j, ("wide", "tm"), 0, 0, tiled=True)
        blk = turned.reshape(wide_parts, tm_parts, chunk_channels, 2 * frames_here, inputs_here)
        if j == 0:
            first, count_sums = correlate(blk, pt, ptr, rm, fm, fmr)
            sums.append(first)
        else:
            sums.append(correlate(blk, pt, ptr, rm)[0])
    sums = jnp.concatenate(sums, axis=0)
    conj_sign = jnp.array([1.0, -1.0], jnp.float32)[None, :, None, None, None]
    vis = unskew(sums, conj_sign)
    local_baselines = NBASE // devices
    send = vis.reshape(local_channels, 2, devices, local_baselines).transpose(2, 0, 1, 3)
    received = lax.all_to_all(send, ("wide", "tm"), 0, 0, tiled=True)
    stacked_in = received.reshape(CH * 2, local_baselines)
    device_position = lax.axis_index("wide") * tm_parts + lax.axis_index("tm")
    global_stack_counts = unskew(count_sums, 1.0).reshape(NBASE)
    local_stack_counts = lax.dynamic_slice_in_dim(
        global_stack_counts, device_position * local_baselines, local_baselines
    )
    delay = delay_matrix_const(CH)
    spectra_out = lax.dot_general(
        stacked_in, delay, (((0,), (0,)), ((), ())), precision=lax.Precision.HIGH,
        preferred_element_type=jnp.float32,
    )
    weight = 1.0 / jnp.sqrt(frames_all * CH * jnp.maximum(local_stack_counts, 1.0))
    return spectra_out.reshape(local_baselines, 2, CH) * weight[:, None, None]


def solution(mesh):
    return jax.shard_map(
        body,
        mesh=mesh,
        in_specs=(P("tm", "wide", None), P(), P()),
        out_specs=P(("wide", "tm"), None, None),
        check_vma=False,
    )
```

```python
import functools
import math

import numpy as np
import jax
import jax.numpy as jnp
from jax import lax
from jax.experimental import pallas as pl
from jax.experimental.pallas import tpu as pltpu
from jax.sharding import PartitionSpec as P

CYL = 4
FEEDS = 256
NSAMP = 2048
CH = 512
CHAN_LO = 256
NBASE = 4096

NT = (((1,), (1,)), ((), ()))


def channel_table_const(length, frequency_channels, first):
    samples_at = np.arange(length, dtype=np.int64)
    channel_at = np.arange(frequency_channels, dtype=np.int64) + first
    turns = (channel_at[:, None] * samples_at[None, :]) % length
    phase = turns.astype(np.float32) * np.float32(2.0 * math.pi / length)
    scale = np.float32(1.0 / math.sqrt(length))
    both = np.stack([np.cos(phase) * scale, -np.sin(phase) * scale], axis=1)
    return both.reshape(2 * frequency_channels, length)


def delay_matrix_const(frequency_channels):
    index = np.arange(frequency_channels, dtype=np.int64)
    phase = ((index[:, None] * index[None, :]) % frequency_channels).astype(np.float32) * np.float32(
        2.0 * math.pi / frequency_channels
    )
    cosine = np.cos(phase).astype(np.float32)
    sine = np.sin(phase).astype(np.float32)
    w = np.zeros((frequency_channels, 2, 2, frequency_channels), np.float32)
    w[:, 0, 0] = cosine
    w[:, 1, 0] = sine
    w[:, 0, 1] = -sine
    w[:, 1, 1] = cosine
    return jnp.asarray(w.reshape(2 * frequency_channels, 2 * frequency_channels))


def pair_keep():
    same = jnp.eye(CYL, dtype=jnp.float32)[:, :, None]
    first = (jnp.arange(FEEDS, dtype=jnp.int32) == 0).astype(jnp.float32)[None, None, :]
    return 1.0 - same * first


def diag_pairs(left, right, upper, write):
    for a in range(CYL):
        for b in range(a, CYL):
            tile = lax.dot_general(
                left[a * FEEDS:(a + 1) * FEEDS], right[b * FEEDS:(b + 1) * FEEDS], NT,
                preferred_element_type=jnp.float32,
            )
            skewed = pltpu.roll(tile, 0, 1, stride=1, stride_axis=0)
            up = jnp.sum(jnp.where(upper, skewed, 0.0), axis=0, keepdims=True)
            write(a * CYL + b, up)
            if a < b:
                total = jnp.sum(skewed, axis=0, keepdims=True)
                write(b * CYL + a, total - up)


def correlate_kernel(*refs, with_counts):
    if with_counts:
        x_ref, pt_ref, ptr_ref, rm_ref, fm_ref, fmr_ref, o_ref, n_ref = refs
    else:
        x_ref, pt_ref, ptr_ref, rm_ref, o_ref = refs
    wide_parts = x_ref.shape[0]
    row_at = lax.broadcasted_iota(jnp.int32, (FEEDS, FEEDS), 0)
    col_at = lax.broadcasted_iota(jnp.int32, (FEEDS, FEEDS), 1)
    upper = col_at >= row_at

    if with_counts:
        @pl.when(pl.program_id(0) == 0)
        def _():
            def write_count(slot, value):
                n_ref[pl.ds(slot, 1), :] = value

            diag_pairs(fm_ref[...], fmr_ref[...], upper, write_count)

    g = None
    gr = None
    for w in range(wide_parts):
        xw = x_ref[w].reshape(-1, x_ref.shape[-1])
        gw = lax.dot_general(pt_ref[w], xw, NT, preferred_element_type=jnp.float32)
        grw = lax.dot_general(ptr_ref[w], xw, NT, preferred_element_type=jnp.float32)
        g = gw if g is None else g + gw
        gr = grw if gr is None else gr + grw
    g = g.astype(jnp.bfloat16)
    gr = gr.astype(jnp.bfloat16)
    yr = jnp.dot(gr, rm_ref[...], preferred_element_type=jnp.float32).astype(jnp.bfloat16)
    for part, right in enumerate((gr, yr)):
        def write_vis(slot, value, part=part):
            o_ref[0, part, pl.ds(slot, 1), :] = value

        diag_pairs(g, right, upper, write_vis)


def correlate(blocks, pt, ptr, rm, fm=None, fmr=None):
    wide_parts, tm_parts, local_channels, rows_each, inputs_each = blocks.shape
    with_counts = fm is not None
    in_specs = [
        pl.BlockSpec((wide_parts, tm_parts, None, rows_each, inputs_each), lambda c: (0, 0, c, 0, 0)),
        pl.BlockSpec(pt.shape, lambda c: (0, 0, 0)),
        pl.BlockSpec(ptr.shape, lambda c: (0, 0, 0)),
        pl.BlockSpec(rm.shape, lambda c: (0, 0)),
    ]
    out_specs = [pl.BlockSpec((1, 2, CYL * CYL, FEEDS), lambda c: (c, 0, 0, 0))]
    out_shape = [jax.ShapeDtypeStruct((local_channels, 2, CYL * CYL, FEEDS), jnp.float32)]
    operands = [blocks, pt, ptr, rm]
    if with_counts:
        in_specs += [pl.BlockSpec(fm.shape, lambda c: (0, 0)), pl.BlockSpec(fmr.shape, lambda c: (0, 0))]
        out_specs.append(pl.BlockSpec((CYL * CYL, FEEDS), lambda c: (0, 0)))
        out_shape.append(jax.ShapeDtypeStruct((CYL * CYL, FEEDS), jnp.float32))
        operands += [fm, fmr]
    positions = CYL * FEEDS
    rows = tm_parts * rows_each
    flops = local_channels * (
        2 * 2 * positions * wide_parts * inputs_each * rows + 2 * positions * rows * rows
        + 20 * 2 * FEEDS * FEEDS * rows
    )
    bytes_accessed = blocks.size * 2 + pt.size * 4 + local_channels * 2 * CYL * CYL * FEEDS * 4
    return pl.pallas_call(
        functools.partial(correlate_kernel, with_counts=with_counts),
        grid=(local_channels,),
        in_specs=in_specs,
        out_specs=out_specs,
        out_shape=out_shape,
        cost_estimate=pl.CostEstimate(flops=flops, transcendentals=0, bytes_accessed=bytes_accessed),
    )(*operands)


def unskew(sums, sign):
    lead = sums.shape[:-2]
    grid = sums.reshape(lead + (CYL, CYL, FEEDS))
    forward = jnp.flip(grid, axis=-1)
    shifted = jnp.roll(grid, 1, axis=-1)
    first_of_pair = jnp.swapaxes(forward, -3, -2)[..., :1]
    k_at = lax.broadcasted_iota(jnp.int32, (CYL, CYL, FEEDS), 2)
    a_at = lax.broadcasted_iota(jnp.int32, (CYL, CYL, FEEDS), 0)
    b_at = lax.broadcasted_iota(jnp.int32, (CYL, CYL, FEEDS), 1)
    backward = jnp.where(k_at == 0, first_of_pair, shifted) * sign
    joined = jnp.where(a_at <= b_at, forward, backward) * pair_keep()
    return joined.reshape(lead + (CYL * CYL, FEEDS))


def body(samples, feed_input_wiring, input_flags):
    frames_here, inputs_here, length = samples.shape
    tm_parts = lax.axis_size("tm")
    wide_parts = lax.axis_size("wide")
    devices = tm_parts * wide_parts
    frames_all = frames_here * tm_parts
    local_channels = CH // devices
    table = channel_table_const(NSAMP, CH, CHAN_LO)
    chunks = math.gcd(2, local_channels)
    chunk_channels = local_channels // chunks
    table = table.reshape(devices, chunks, chunk_channels * 2, length).transpose(1, 0, 2, 3)
    table = jnp.asarray(table.reshape(chunks, devices * chunk_channels * 2, length), dtype=jnp.bfloat16)
    flattened = samples.reshape(frames_here * inputs_here, length)
    chunk_rows = devices * chunk_channels * 2
    table = table.reshape(chunks * chunk_rows, length)

    def channelize(rows):
        spectra = lax.dot_general(rows, flattened, NT, preferred_element_type=jnp.float32)
        return spectra.astype(jnp.bfloat16).reshape(-1, devices, chunk_channels, 2 * frames_here, inputs_here)

    spectra = [channelize(table[:chunk_rows])[0]]
    if chunks > 1:
        rest = channelize(table[chunk_rows:])
        spectra += [rest[j] for j in range(chunks - 1)]

    inputs_all = wide_parts * inputs_here
    flags = input_flags.astype(jnp.bfloat16)
    source = jnp.arange(inputs_all, dtype=jnp.int32)
    wiring_rev = jnp.flip(feed_input_wiring.reshape(CYL, FEEDS), axis=1).reshape(CYL * FEEDS)
    pt_full = jnp.where(feed_input_wiring[:, None] == source[None, :], flags[None, :], jnp.bfloat16(0))
    ptr_full = jnp.where(wiring_rev[:, None] == source[None, :], flags[None, :], jnp.bfloat16(0))
    first_lane = (lax.broadcasted_iota(jnp.int32, (CYL * FEEDS, 128), 1) == 0).astype(jnp.bfloat16)
    fm = jnp.sum(pt_full.astype(jnp.float32), axis=1).astype(jnp.bfloat16)[:, None] * first_lane
    fmr = jnp.sum(ptr_full.astype(jnp.float32), axis=1).astype(jnp.bfloat16)[:, None] * first_lane
    pt = pt_full.reshape(CYL * FEEDS, wide_parts, inputs_here).transpose(1, 0, 2)
    ptr = ptr_full.reshape(CYL * FEEDS, wide_parts, inputs_here).transpose(1, 0, 2)

    rows = tm_parts * 2 * frames_here
    r_at = np.arange(rows)
    frame_at = r_at % frames_here
    part_at = (r_at // frames_here) % 2
    group_at = r_at // (2 * frames_here)
    rm = np.zeros((rows, rows), np.float32)
    for r in range(rows):
        partner = group_at[r] * 2 * frames_here + (1 - part_at[r]) * frames_here + frame_at[r]
        rm[partner, r] = -1.0 if part_at[r] == 0 else 1.0
    rm = jnp.asarray(rm, dtype=jnp.bfloat16)

    local_baselines = NBASE // devices
    conj_sign = jnp.array([1.0, -1.0], jnp.float32)[None, :, None, None, None]

    def send_of(chunk_sums):
        vis = unskew(chunk_sums, conj_sign)
        return vis.reshape(chunk_channels, 2, devices, local_baselines).transpose(2, 0, 1, 3)

    sums = []
    received = []
    for j in range(chunks):
        spectra_j = spectra[j]
        if j >= 2:
            spectra_j, _ = lax.optimization_barrier((spectra_j, sums[j - 2]))
        elif j == 1:
            spectra_j, pt, ptr, fm, fmr = lax.optimization_barrier((spectra_j, pt, ptr, fm, fmr))
        turned = lax.all_to_all(spectra_j, ("wide", "tm"), 0, 0, tiled=True)
        blk = turned.reshape(wide_parts, tm_parts, chunk_channels, 2 * frames_here, inputs_here)
        if j >= 1:
            blk, send_prev = lax.optimization_barrier((blk, send_of(sums[j - 1])))
            received.append(lax.all_to_all(send_prev, ("wide", "tm"), 0, 0, tiled=True))
        if j == 0:
            first, count_sums = correlate(blk, pt, ptr, rm, fm, fmr)
            sums.append(first)
        else:
            sums.append(correlate(blk, pt, ptr, rm)[0])
    received.append(lax.all_to_all(send_of(sums[-1]), ("wide", "tm"), 0, 0, tiled=True))
    stacked_in = jnp.stack(received, axis=1).reshape(CH * 2, local_baselines)
    device_position = lax.axis_index("wide") * tm_parts + lax.axis_index("tm")
    global_stack_counts = unskew(count_sums, 1.0).reshape(NBASE)
    local_stack_counts = lax.dynamic_slice_in_dim(
        global_stack_counts, device_position * local_baselines, local_baselines
    )
    delay = delay_matrix_const(CH)
    spectra_out = lax.dot_general(
        stacked_in, delay, (((0,), (0,)), ((), ())), precision=lax.Precision.HIGH,
        preferred_element_type=jnp.float32,
    )
    weight = 1.0 / jnp.sqrt(frames_all * CH * jnp.maximum(local_stack_counts, 1.0))
    return spectra_out.reshape(local_baselines, 2, CH) * weight[:, None, None]


def solution(mesh):
    return jax.shard_map(
        body,
        mesh=mesh,
        in_specs=(P("tm", "wide", None), P(), P()),
        out_specs=P(("wide", "tm"), None, None),
        check_vma=False,
    )
```

```python
import functools
import math

import numpy as np
import jax
import jax.numpy as jnp
from jax import lax
from jax.experimental import pallas as pl
from jax.experimental.pallas import tpu as pltpu
from jax.sharding import PartitionSpec as P

CYL = 4
FEEDS = 256
NSAMP = 2048
CH = 512
CHAN_LO = 256
NBASE = 4096

NT = (((1,), (1,)), ((), ()))


def channel_table_const(length, frequency_channels, first):
    samples_at = np.arange(length, dtype=np.int64)
    channel_at = np.arange(frequency_channels, dtype=np.int64) + first
    turns = (channel_at[:, None] * samples_at[None, :]) % length
    phase = turns.astype(np.float32) * np.float32(2.0 * math.pi / length)
    scale = np.float32(1.0 / math.sqrt(length))
    both = np.stack([np.cos(phase) * scale, -np.sin(phase) * scale], axis=1)
    return both.reshape(2 * frequency_channels, length)


def delay_matrix_const(frequency_channels):
    index = np.arange(frequency_channels, dtype=np.int64)
    phase = ((index[:, None] * index[None, :]) % frequency_channels).astype(np.float32) * np.float32(
        2.0 * math.pi / frequency_channels
    )
    cosine = np.cos(phase).astype(np.float32)
    sine = np.sin(phase).astype(np.float32)
    w = np.zeros((frequency_channels, 2, 2, frequency_channels), np.float32)
    w[:, 0, 0] = cosine
    w[:, 1, 0] = sine
    w[:, 0, 1] = -sine
    w[:, 1, 1] = cosine
    return jnp.asarray(w.reshape(2 * frequency_channels, 2 * frequency_channels))


def pair_keep():
    same = jnp.eye(CYL, dtype=jnp.float32)[:, :, None]
    first = (jnp.arange(FEEDS, dtype=jnp.int32) == 0).astype(jnp.float32)[None, None, :]
    return 1.0 - same * first


def diag_pairs(left, right, upper, write):
    for a in range(CYL):
        for b in range(a, CYL):
            tile = lax.dot_general(
                left[a * FEEDS:(a + 1) * FEEDS], right[b * FEEDS:(b + 1) * FEEDS], NT,
                preferred_element_type=jnp.float32,
            )
            skewed = pltpu.roll(tile, 0, 1, stride=1, stride_axis=0)
            up = jnp.sum(jnp.where(upper, skewed, 0.0), axis=0, keepdims=True)
            write(a * CYL + b, up)
            if a < b:
                total = jnp.sum(skewed, axis=0, keepdims=True)
                write(b * CYL + a, total - up)


def correlate_kernel(*refs, with_counts):
    if with_counts:
        x_ref, pt_ref, ptr_ref, rm_ref, fm_ref, fmr_ref, o_ref, n_ref = refs
    else:
        x_ref, pt_ref, ptr_ref, rm_ref, o_ref = refs
    wide_parts = x_ref.shape[0]
    row_at = lax.broadcasted_iota(jnp.int32, (FEEDS, FEEDS), 0)
    col_at = lax.broadcasted_iota(jnp.int32, (FEEDS, FEEDS), 1)
    upper = col_at >= row_at

    if with_counts:
        @pl.when(pl.program_id(0) == 0)
        def _():
            def write_count(slot, value):
                n_ref[pl.ds(slot, 1), :] = value

            diag_pairs(fm_ref[...], fmr_ref[...], upper, write_count)

    g = None
    gr = None
    for w in range(wide_parts):
        xw = x_ref[w].reshape(-1, x_ref.shape[-1])
        gw = lax.dot_general(pt_ref[w], xw, NT, preferred_element_type=jnp.float32)
        grw = lax.dot_general(ptr_ref[w], xw, NT, preferred_element_type=jnp.float32)
        g = gw if g is None else g + gw
        gr = grw if gr is None else gr + grw
    g = g.astype(jnp.bfloat16)
    gr = gr.astype(jnp.bfloat16)
    yr = jnp.dot(gr, rm_ref[...], preferred_element_type=jnp.float32).astype(jnp.bfloat16)
    for part, right in enumerate((gr, yr)):
        def write_vis(slot, value, part=part):
            o_ref[0, part, pl.ds(slot, 1), :] = value

        diag_pairs(g, right, upper, write_vis)


def correlate(blocks, pt, ptr, rm, fm=None, fmr=None):
    wide_parts, tm_parts, local_channels, rows_each, inputs_each = blocks.shape
    with_counts = fm is not None
    in_specs = [
        pl.BlockSpec((wide_parts, tm_parts, None, rows_each, inputs_each), lambda c: (0, 0, c, 0, 0)),
        pl.BlockSpec(pt.shape, lambda c: (0, 0, 0)),
        pl.BlockSpec(ptr.shape, lambda c: (0, 0, 0)),
        pl.BlockSpec(rm.shape, lambda c: (0, 0)),
    ]
    out_specs = [pl.BlockSpec((1, 2, CYL * CYL, FEEDS), lambda c: (c, 0, 0, 0))]
    out_shape = [jax.ShapeDtypeStruct((local_channels, 2, CYL * CYL, FEEDS), jnp.float32)]
    operands = [blocks, pt, ptr, rm]
    if with_counts:
        in_specs += [pl.BlockSpec(fm.shape, lambda c: (0, 0)), pl.BlockSpec(fmr.shape, lambda c: (0, 0))]
        out_specs.append(pl.BlockSpec((CYL * CYL, FEEDS), lambda c: (0, 0)))
        out_shape.append(jax.ShapeDtypeStruct((CYL * CYL, FEEDS), jnp.float32))
        operands += [fm, fmr]
    positions = CYL * FEEDS
    rows = tm_parts * rows_each
    flops = local_channels * (
        2 * 2 * positions * wide_parts * inputs_each * rows + 2 * positions * rows * rows
        + 20 * 2 * FEEDS * FEEDS * rows
    )
    bytes_accessed = blocks.size * 2 + pt.size * 4 + local_channels * 2 * CYL * CYL * FEEDS * 4
    return pl.pallas_call(
        functools.partial(correlate_kernel, with_counts=with_counts),
        grid=(local_channels,),
        in_specs=in_specs,
        out_specs=out_specs,
        out_shape=out_shape,
        cost_estimate=pl.CostEstimate(flops=flops, transcendentals=0, bytes_accessed=bytes_accessed),
    )(*operands)


def unskew(sums, sign):
    lead = sums.shape[:-2]
    grid = sums.reshape(lead + (CYL, CYL, FEEDS))
    forward = jnp.flip(grid, axis=-1)
    shifted = jnp.roll(grid, 1, axis=-1)
    first_of_pair = jnp.swapaxes(forward, -3, -2)[..., :1]
    k_at = lax.broadcasted_iota(jnp.int32, (CYL, CYL, FEEDS), 2)
    a_at = lax.broadcasted_iota(jnp.int32, (CYL, CYL, FEEDS), 0)
    b_at = lax.broadcasted_iota(jnp.int32, (CYL, CYL, FEEDS), 1)
    backward = jnp.where(k_at == 0, first_of_pair, shifted) * sign
    joined = jnp.where(a_at <= b_at, forward, backward) * pair_keep()
    return joined.reshape(lead + (CYL * CYL, FEEDS))


def body(samples, feed_input_wiring, input_flags):
    frames_here, inputs_here, length = samples.shape
    tm_parts = lax.axis_size("tm")
    wide_parts = lax.axis_size("wide")
    devices = tm_parts * wide_parts
    frames_all = frames_here * tm_parts
    local_channels = CH // devices
    table = channel_table_const(NSAMP, CH, CHAN_LO)
    chunks = math.gcd(2, local_channels)
    chunk_channels = local_channels // chunks
    table = table.reshape(devices, chunks, chunk_channels * 2, length).transpose(1, 0, 2, 3)
    table = jnp.asarray(table.reshape(chunks, devices * chunk_channels * 2, length), dtype=jnp.bfloat16)
    flattened = samples.reshape(frames_here * inputs_here, length)
    chunk_rows = devices * chunk_channels * 2
    table = table.reshape(chunks * chunk_rows, length)

    def channelize(rows):
        spectra = lax.dot_general(rows, flattened, NT, preferred_element_type=jnp.float32)
        return spectra.astype(jnp.bfloat16).reshape(-1, devices, chunk_channels, 2 * frames_here, inputs_here)

    spectra = [channelize(table[:chunk_rows])[0]]
    if chunks > 1:
        rest = channelize(table[chunk_rows:])
        spectra += [rest[j] for j in range(chunks - 1)]

    inputs_all = wide_parts * inputs_here
    flags = input_flags.astype(jnp.bfloat16)
    source = jnp.arange(inputs_all, dtype=jnp.int32)
    wiring_rev = jnp.flip(feed_input_wiring.reshape(CYL, FEEDS), axis=1).reshape(CYL * FEEDS)
    pt_full = jnp.where(feed_input_wiring[:, None] == source[None, :], flags[None, :], jnp.bfloat16(0))
    ptr_full = jnp.where(wiring_rev[:, None] == source[None, :], flags[None, :], jnp.bfloat16(0))
    first_lane = (lax.broadcasted_iota(jnp.int32, (CYL * FEEDS, 128), 1) == 0).astype(jnp.bfloat16)
    fm = jnp.sum(pt_full.astype(jnp.float32), axis=1).astype(jnp.bfloat16)[:, None] * first_lane
    fmr = jnp.sum(ptr_full.astype(jnp.float32), axis=1).astype(jnp.bfloat16)[:, None] * first_lane
    pt = pt_full.reshape(CYL * FEEDS, wide_parts, inputs_here).transpose(1, 0, 2)
    ptr = ptr_full.reshape(CYL * FEEDS, wide_parts, inputs_here).transpose(1, 0, 2)

    rows = tm_parts * 2 * frames_here
    r_at = np.arange(rows)
    frame_at = r_at % frames_here
    part_at = (r_at // frames_here) % 2
    group_at = r_at // (2 * frames_here)
    rm = np.zeros((rows, rows), np.float32)
    for r in range(rows):
        partner = group_at[r] * 2 * frames_here + (1 - part_at[r]) * frames_here + frame_at[r]
        rm[partner, r] = -1.0 if part_at[r] == 0 else 1.0
    rm = jnp.asarray(rm, dtype=jnp.bfloat16)

    sums = []
    for j in range(chunks):
        spectra_j = spectra[j]
        if j >= 2:
            spectra_j, _ = lax.optimization_barrier((spectra_j, sums[j - 2]))
        elif j == 1:
            spectra_j, pt, ptr, fm, fmr = lax.optimization_barrier((spectra_j, pt, ptr, fm, fmr))
        turned = lax.all_to_all(spectra_j, ("wide", "tm"), 0, 0, tiled=True)
        blk = turned.reshape(wide_parts, tm_parts, chunk_channels, 2 * frames_here, inputs_here)
        if j == 0:
            first, count_sums = correlate(blk, pt, ptr, rm, fm, fmr)
            sums.append(first)
        else:
            sums.append(correlate(blk, pt, ptr, rm)[0])
    sums = jnp.concatenate(sums, axis=0)
    conj_sign = jnp.array([1.0, -1.0], jnp.float32)[None, :, None, None, None]
    vis = unskew(sums, conj_sign)
    local_baselines = NBASE // devices
    send = vis.reshape(local_channels, 2, devices, local_baselines).transpose(2, 0, 1, 3)
    received = lax.all_to_all(send.astype(jnp.bfloat16), ("wide", "tm"), 0, 0, tiled=True)
    stacked_in = received.astype(jnp.float32).reshape(CH * 2, local_baselines)
    device_position = lax.axis_index("wide") * tm_parts + lax.axis_index("tm")
    global_stack_counts = unskew(count_sums, 1.0).reshape(NBASE)
    local_stack_counts = lax.dynamic_slice_in_dim(
        global_stack_counts, device_position * local_baselines, local_baselines
    )
    delay = delay_matrix_const(CH)
    spectra_out = lax.dot_general(
        stacked_in, delay, (((0,), (0,)), ((), ())), precision=lax.Precision.HIGH,
        preferred_element_type=jnp.float32,
    )
    weight = 1.0 / jnp.sqrt(frames_all * CH * jnp.maximum(local_stack_counts, 1.0))
    return spectra_out.reshape(local_baselines, 2, CH) * weight[:, None, None]


def solution(mesh):
    return jax.shard_map(
        body,
        mesh=mesh,
        in_specs=(P("tm", "wide", None), P(), P()),
        out_specs=P(("wide", "tm"), None, None),
        check_vma=False,
    )
```

```python
import functools
import math

import ml_dtypes
import numpy as np
import jax
import jax.numpy as jnp
from jax import lax
from jax.experimental import pallas as pl
from jax.experimental.pallas import tpu as pltpu
from jax.sharding import PartitionSpec as P

CYL = 4
FEEDS = 256
NSAMP = 2048
CH = 512
CHAN_LO = 256
NBASE = 4096

NT = (((1,), (1,)), ((), ()))


def channel_table_const(length, frequency_channels, first):
    samples_at = np.arange(length, dtype=np.int64)
    channel_at = np.arange(frequency_channels, dtype=np.int64) + first
    turns = (channel_at[:, None] * samples_at[None, :]) % length
    phase = turns.astype(np.float32) * np.float32(2.0 * math.pi / length)
    scale = np.float32(1.0 / math.sqrt(length))
    both = np.stack([np.cos(phase) * scale, -np.sin(phase) * scale], axis=1)
    return both.reshape(2 * frequency_channels, length)


def delay_matrix_const(frequency_channels):
    index = np.arange(frequency_channels, dtype=np.int64)
    phase = ((index[:, None] * index[None, :]) % frequency_channels).astype(np.float32) * np.float32(
        2.0 * math.pi / frequency_channels
    )
    cosine = np.cos(phase).astype(np.float32)
    sine = np.sin(phase).astype(np.float32)
    w = np.zeros((frequency_channels, 2, 2, frequency_channels), np.float32)
    w[:, 0, 0] = cosine
    w[:, 1, 0] = sine
    w[:, 0, 1] = -sine
    w[:, 1, 1] = cosine
    return w.reshape(2 * frequency_channels, 2 * frequency_channels)


def pair_keep():
    same = jnp.eye(CYL, dtype=jnp.float32)[:, :, None]
    first = (jnp.arange(FEEDS, dtype=jnp.int32) == 0).astype(jnp.float32)[None, None, :]
    return 1.0 - same * first


def diag_pairs(left, right, upper, write):
    for a in range(CYL):
        for b in range(a, CYL):
            tile = lax.dot_general(
                left[a * FEEDS:(a + 1) * FEEDS], right[b * FEEDS:(b + 1) * FEEDS], NT,
                preferred_element_type=jnp.float32,
            )
            skewed = pltpu.roll(tile, 0, 1, stride=1, stride_axis=0)
            up = jnp.sum(jnp.where(upper, skewed, 0.0), axis=0, keepdims=True)
            write(a * CYL + b, up)
            if a < b:
                total = jnp.sum(skewed, axis=0, keepdims=True)
                write(b * CYL + a, total - up)


def correlate_kernel(*refs, with_counts):
    if with_counts:
        x_ref, pt_ref, ptr_ref, rm_ref, fm_ref, fmr_ref, o_ref, n_ref = refs
    else:
        x_ref, pt_ref, ptr_ref, rm_ref, o_ref = refs
    wide_parts = x_ref.shape[0]
    row_at = lax.broadcasted_iota(jnp.int32, (FEEDS, FEEDS), 0)
    col_at = lax.broadcasted_iota(jnp.int32, (FEEDS, FEEDS), 1)
    upper = col_at >= row_at

    if with_counts:
        @pl.when(pl.program_id(0) == 0)
        def _():
            def write_count(slot, value):
                n_ref[pl.ds(slot, 1), :] = value

            diag_pairs(fm_ref[...], fmr_ref[...], upper, write_count)

    g = None
    gr = None
    for w in range(wide_parts):
        xw = x_ref[w].reshape(-1, x_ref.shape[-1])
        gw = lax.dot_general(pt_ref[w], xw, NT, preferred_element_type=jnp.float32)
        grw = lax.dot_general(ptr_ref[w], xw, NT, preferred_element_type=jnp.float32)
        g = gw if g is None else g + gw
        gr = grw if gr is None else gr + grw
    g = g.astype(jnp.bfloat16)
    gr = gr.astype(jnp.bfloat16)
    yr = jnp.dot(gr, rm_ref[...], preferred_element_type=jnp.float32).astype(jnp.bfloat16)
    for part, right in enumerate((gr, yr)):
        def write_vis(slot, value, part=part):
            o_ref[0, part, pl.ds(slot, 1), :] = value

        diag_pairs(g, right, upper, write_vis)


def correlate(blocks, pt, ptr, rm, fm=None, fmr=None):
    wide_parts, tm_parts, local_channels, rows_each, inputs_each = blocks.shape
    with_counts = fm is not None
    in_specs = [
        pl.BlockSpec((wide_parts, tm_parts, None, rows_each, inputs_each), lambda c: (0, 0, c, 0, 0)),
        pl.BlockSpec(pt.shape, lambda c: (0, 0, 0)),
        pl.BlockSpec(ptr.shape, lambda c: (0, 0, 0)),
        pl.BlockSpec(rm.shape, lambda c: (0, 0)),
    ]
    out_specs = [pl.BlockSpec((1, 2, CYL * CYL, FEEDS), lambda c: (c, 0, 0, 0))]
    out_shape = [jax.ShapeDtypeStruct((local_channels, 2, CYL * CYL, FEEDS), jnp.float32)]
    operands = [blocks, pt, ptr, rm]
    if with_counts:
        in_specs += [pl.BlockSpec(fm.shape, lambda c: (0, 0)), pl.BlockSpec(fmr.shape, lambda c: (0, 0))]
        out_specs.append(pl.BlockSpec((CYL * CYL, FEEDS), lambda c: (0, 0)))
        out_shape.append(jax.ShapeDtypeStruct((CYL * CYL, FEEDS), jnp.float32))
        operands += [fm, fmr]
    positions = CYL * FEEDS
    rows = tm_parts * rows_each
    flops = local_channels * (
        2 * 2 * positions * wide_parts * inputs_each * rows + 2 * positions * rows * rows
        + 20 * 2 * FEEDS * FEEDS * rows
    )
    bytes_accessed = blocks.size * 2 + pt.size * 4 + local_channels * 2 * CYL * CYL * FEEDS * 4
    return pl.pallas_call(
        functools.partial(correlate_kernel, with_counts=with_counts),
        grid=(local_channels,),
        in_specs=in_specs,
        out_specs=out_specs,
        out_shape=out_shape,
        cost_estimate=pl.CostEstimate(flops=flops, transcendentals=0, bytes_accessed=bytes_accessed),
    )(*operands)


def unskew(sums, sign):
    lead = sums.shape[:-2]
    grid = sums.reshape(lead + (CYL, CYL, FEEDS))
    forward = jnp.flip(grid, axis=-1)
    shifted = jnp.roll(grid, 1, axis=-1)
    first_of_pair = jnp.swapaxes(forward, -3, -2)[..., :1]
    k_at = lax.broadcasted_iota(jnp.int32, (CYL, CYL, FEEDS), 2)
    a_at = lax.broadcasted_iota(jnp.int32, (CYL, CYL, FEEDS), 0)
    b_at = lax.broadcasted_iota(jnp.int32, (CYL, CYL, FEEDS), 1)
    backward = jnp.where(k_at == 0, first_of_pair, shifted) * sign
    joined = jnp.where(a_at <= b_at, forward, backward) * pair_keep()
    return joined.reshape(lead + (CYL * CYL, FEEDS))


def body(samples, feed_input_wiring, input_flags):
    frames_here, inputs_here, length = samples.shape
    tm_parts = lax.axis_size("tm")
    wide_parts = lax.axis_size("wide")
    devices = tm_parts * wide_parts
    frames_all = frames_here * tm_parts
    local_channels = CH // devices
    table = channel_table_const(NSAMP, CH, CHAN_LO)
    chunks = math.gcd(2, local_channels)
    chunk_channels = local_channels // chunks
    table = table.reshape(devices, chunks, chunk_channels * 2, length).transpose(1, 0, 2, 3)
    table = jnp.asarray(table.reshape(chunks, devices * chunk_channels * 2, length), dtype=jnp.bfloat16)
    flattened = samples.reshape(frames_here * inputs_here, length)
    chunk_rows = devices * chunk_channels * 2
    table = table.reshape(chunks * chunk_rows, length)

    def channelize(rows):
        spectra = lax.dot_general(rows, flattened, NT, preferred_element_type=jnp.float32)
        return spectra.astype(jnp.bfloat16).reshape(-1, devices, chunk_channels, 2 * frames_here, inputs_here)

    spectra = [channelize(table[:chunk_rows])[0]]
    if chunks > 1:
        rest = channelize(table[chunk_rows:])
        spectra += [rest[j] for j in range(chunks - 1)]

    inputs_all = wide_parts * inputs_here
    flags = input_flags.astype(jnp.bfloat16)
    source = jnp.arange(inputs_all, dtype=jnp.int32)
    wiring_rev = jnp.flip(feed_input_wiring.reshape(CYL, FEEDS), axis=1).reshape(CYL * FEEDS)
    pt_full = jnp.where(feed_input_wiring[:, None] == source[None, :], flags[None, :], jnp.bfloat16(0))
    ptr_full = jnp.where(wiring_rev[:, None] == source[None, :], flags[None, :], jnp.bfloat16(0))
    first_lane = (lax.broadcasted_iota(jnp.int32, (CYL * FEEDS, 128), 1) == 0).astype(jnp.bfloat16)
    fm = jnp.sum(pt_full.astype(jnp.float32), axis=1).astype(jnp.bfloat16)[:, None] * first_lane
    fmr = jnp.sum(ptr_full.astype(jnp.float32), axis=1).astype(jnp.bfloat16)[:, None] * first_lane
    pt = pt_full.reshape(CYL * FEEDS, wide_parts, inputs_here).transpose(1, 0, 2)
    ptr = ptr_full.reshape(CYL * FEEDS, wide_parts, inputs_here).transpose(1, 0, 2)

    rows = tm_parts * 2 * frames_here
    r_at = np.arange(rows)
    frame_at = r_at % frames_here
    part_at = (r_at // frames_here) % 2
    group_at = r_at // (2 * frames_here)
    rm = np.zeros((rows, rows), np.float32)
    for r in range(rows):
        partner = group_at[r] * 2 * frames_here + (1 - part_at[r]) * frames_here + frame_at[r]
        rm[partner, r] = -1.0 if part_at[r] == 0 else 1.0
    rm = jnp.asarray(rm, dtype=jnp.bfloat16)

    sums = []
    for j in range(chunks):
        spectra_j = spectra[j]
        if j >= 2:
            spectra_j, _ = lax.optimization_barrier((spectra_j, sums[j - 2]))
        elif j == 1:
            spectra_j, pt, ptr, fm, fmr = lax.optimization_barrier((spectra_j, pt, ptr, fm, fmr))
        turned = lax.all_to_all(spectra_j, ("wide", "tm"), 0, 0, tiled=True)
        blk = turned.reshape(wide_parts, tm_parts, chunk_channels, 2 * frames_here, inputs_here)
        if j == 0:
            first, count_sums = correlate(blk, pt, ptr, rm, fm, fmr)
            sums.append(first)
        else:
            sums.append(correlate(blk, pt, ptr, rm)[0])
    sums = jnp.concatenate(sums, axis=0)
    conj_sign = jnp.array([1.0, -1.0], jnp.float32)[None, :, None, None, None]
    vis = unskew(sums, conj_sign)
    local_baselines = NBASE // devices
    send = vis.reshape(local_channels, 2, devices, local_baselines).transpose(2, 0, 1, 3)
    received = lax.all_to_all(send.astype(jnp.bfloat16), ("wide", "tm"), 0, 0, tiled=True)
    stacked_in = received.reshape(CH * 2, local_baselines)
    device_position = lax.axis_index("wide") * tm_parts + lax.axis_index("tm")
    global_stack_counts = unskew(count_sums, 1.0).reshape(NBASE)
    local_stack_counts = lax.dynamic_slice_in_dim(
        global_stack_counts, device_position * local_baselines, local_baselines
    )
    delay = delay_matrix_const(CH)
    high_np = delay.astype(ml_dtypes.bfloat16)
    delay_high = jnp.asarray(high_np)
    delay_low = jnp.asarray((delay - high_np.astype(np.float32)).astype(ml_dtypes.bfloat16))
    contract = (((0,), (0,)), ((), ()))
    spectra_out = lax.dot_general(
        stacked_in, delay_high, contract, preferred_element_type=jnp.float32
    ) + lax.dot_general(stacked_in, delay_low, contract, preferred_element_type=jnp.float32)
    weight = 1.0 / jnp.sqrt(frames_all * CH * jnp.maximum(local_stack_counts, 1.0))
    return spectra_out.reshape(local_baselines, 2, CH) * weight[:, None, None]


def solution(mesh):
    return jax.shard_map(
        body,
        mesh=mesh,
        in_specs=(P("tm", "wide", None), P(), P()),
        out_specs=P(("wide", "tm"), None, None),
        check_vma=False,
    )
```

```python
import functools
import math

import numpy as np
import jax
import jax.numpy as jnp
from jax import lax
from jax.experimental import pallas as pl
from jax.experimental.pallas import tpu as pltpu
from jax.sharding import PartitionSpec as P

CYL = 4
FEEDS = 256
NSAMP = 2048
CH = 512
CHAN_LO = 256
NBASE = 4096

NT = (((1,), (1,)), ((), ()))


def channel_table_const(length, frequency_channels, first):
    samples_at = np.arange(length, dtype=np.int64)
    channel_at = np.arange(frequency_channels, dtype=np.int64) + first
    turns = (channel_at[:, None] * samples_at[None, :]) % length
    phase = turns.astype(np.float32) * np.float32(2.0 * math.pi / length)
    scale = np.float32(1.0 / math.sqrt(length))
    both = np.stack([np.cos(phase) * scale, -np.sin(phase) * scale], axis=1)
    return both.reshape(2 * frequency_channels, length)


def delay_matrix_const(frequency_channels):
    index = np.arange(frequency_channels, dtype=np.int64)
    phase = ((index[:, None] * index[None, :]) % frequency_channels).astype(np.float32) * np.float32(
        2.0 * math.pi / frequency_channels
    )
    cosine = np.cos(phase).astype(np.float32)
    sine = np.sin(phase).astype(np.float32)
    w = np.zeros((frequency_channels, 2, 2, frequency_channels), np.float32)
    w[:, 0, 0] = cosine
    w[:, 1, 0] = sine
    w[:, 0, 1] = -sine
    w[:, 1, 1] = cosine
    return jnp.asarray(w.reshape(2 * frequency_channels, 2 * frequency_channels))


def pair_keep():
    same = jnp.eye(CYL, dtype=jnp.float32)[:, :, None]
    first = (jnp.arange(FEEDS, dtype=jnp.int32) == 0).astype(jnp.float32)[None, None, :]
    return 1.0 - same * first


HALF = FEEDS // 2


def diag_pairs(left, right, upper, upper_half, write):
    for a in range(CYL):
        for b in range(a, CYL):
            right_b = right[b * FEEDS:(b + 1) * FEEDS]
            if a == b:
                top = lax.dot_general(
                    left[a * FEEDS:a * FEEDS + HALF], right_b, NT, preferred_element_type=jnp.float32
                )
                top = pltpu.roll(top, 0, 1, stride=1, stride_axis=0)
                bottom = lax.dot_general(
                    left[a * FEEDS + HALF:(a + 1) * FEEDS], right_b[:HALF], NT,
                    preferred_element_type=jnp.float32,
                )
                bottom = pltpu.roll(bottom, 0, 1, stride=1, stride_axis=0)
                up_left = jnp.sum(jnp.where(upper_half, top[:, :HALF], 0.0), axis=0, keepdims=True)
                up_right = jnp.sum(top[:, HALF:], axis=0, keepdims=True) + jnp.sum(
                    jnp.where(upper_half, bottom, 0.0), axis=0, keepdims=True
                )
                write(a * CYL + b, jnp.concatenate([up_left, up_right], axis=1))
                continue
            tile = lax.dot_general(
                left[a * FEEDS:(a + 1) * FEEDS], right_b, NT, preferred_element_type=jnp.float32,
            )
            skewed = pltpu.roll(tile, 0, 1, stride=1, stride_axis=0)
            up = jnp.sum(jnp.where(upper, skewed, 0.0), axis=0, keepdims=True)
            write(a * CYL + b, up)
            total = jnp.sum(skewed, axis=0, keepdims=True)
            write(b * CYL + a, total - up)


def correlate_kernel(*refs, with_counts):
    if with_counts:
        x_ref, pt_ref, ptr_ref, rm_ref, fm_ref, fmr_ref, o_ref, n_ref = refs
    else:
        x_ref, pt_ref, ptr_ref, rm_ref, o_ref = refs
    wide_parts = x_ref.shape[0]
    row_at = lax.broadcasted_iota(jnp.int32, (FEEDS, FEEDS), 0)
    col_at = lax.broadcasted_iota(jnp.int32, (FEEDS, FEEDS), 1)
    upper = col_at >= row_at
    upper_half = upper[:HALF, :HALF]

    if with_counts:
        @pl.when(pl.program_id(0) == 0)
        def _():
            def write_count(slot, value):
                n_ref[pl.ds(slot, 1), :] = value

            diag_pairs(fm_ref[...], fmr_ref[...], upper, upper_half, write_count)

    g = None
    gr = None
    for w in range(wide_parts):
        xw = x_ref[w].reshape(-1, x_ref.shape[-1])
        gw = lax.dot_general(pt_ref[w], xw, NT, preferred_element_type=jnp.float32)
        grw = lax.dot_general(ptr_ref[w], xw, NT, preferred_element_type=jnp.float32)
        g = gw if g is None else g + gw
        gr = grw if gr is None else gr + grw
    g = g.astype(jnp.bfloat16)
    gr = gr.astype(jnp.bfloat16)
    yr = jnp.dot(gr, rm_ref[...], preferred_element_type=jnp.float32).astype(jnp.bfloat16)
    for part, right in enumerate((gr, yr)):
        def write_vis(slot, value, part=part):
            o_ref[0, part, pl.ds(slot, 1), :] = value

        diag_pairs(g, right, upper, upper_half, write_vis)


def correlate(blocks, pt, ptr, rm, fm=None, fmr=None):
    wide_parts, tm_parts, local_channels, rows_each, inputs_each = blocks.shape
    with_counts = fm is not None
    in_specs = [
        pl.BlockSpec((wide_parts, tm_parts, None, rows_each, inputs_each), lambda c: (0, 0, c, 0, 0)),
        pl.BlockSpec(pt.shape, lambda c: (0, 0, 0)),
        pl.BlockSpec(ptr.shape, lambda c: (0, 0, 0)),
        pl.BlockSpec(rm.shape, lambda c: (0, 0)),
    ]
    out_specs = [pl.BlockSpec((1, 2, CYL * CYL, FEEDS), lambda c: (c, 0, 0, 0))]
    out_shape = [jax.ShapeDtypeStruct((local_channels, 2, CYL * CYL, FEEDS), jnp.float32)]
    operands = [blocks, pt, ptr, rm]
    if with_counts:
        in_specs += [pl.BlockSpec(fm.shape, lambda c: (0, 0)), pl.BlockSpec(fmr.shape, lambda c: (0, 0))]
        out_specs.append(pl.BlockSpec((CYL * CYL, FEEDS), lambda c: (0, 0)))
        out_shape.append(jax.ShapeDtypeStruct((CYL * CYL, FEEDS), jnp.float32))
        operands += [fm, fmr]
    positions = CYL * FEEDS
    rows = tm_parts * rows_each
    flops = local_channels * (
        2 * 2 * positions * wide_parts * inputs_each * rows + 2 * positions * rows * rows
        + 20 * 2 * FEEDS * FEEDS * rows
    )
    bytes_accessed = blocks.size * 2 + pt.size * 4 + local_channels * 2 * CYL * CYL * FEEDS * 4
    return pl.pallas_call(
        functools.partial(correlate_kernel, with_counts=with_counts),
        grid=(local_channels,),
        in_specs=in_specs,
        out_specs=out_specs,
        out_shape=out_shape,
        cost_estimate=pl.CostEstimate(flops=flops, transcendentals=0, bytes_accessed=bytes_accessed),
    )(*operands)


def unskew(sums, sign):
    lead = sums.shape[:-2]
    grid = sums.reshape(lead + (CYL, CYL, FEEDS))
    forward = jnp.flip(grid, axis=-1)
    shifted = jnp.roll(grid, 1, axis=-1)
    first_of_pair = jnp.swapaxes(forward, -3, -2)[..., :1]
    k_at = lax.broadcasted_iota(jnp.int32, (CYL, CYL, FEEDS), 2)
    a_at = lax.broadcasted_iota(jnp.int32, (CYL, CYL, FEEDS), 0)
    b_at = lax.broadcasted_iota(jnp.int32, (CYL, CYL, FEEDS), 1)
    backward = jnp.where(k_at == 0, first_of_pair, shifted) * sign
    joined = jnp.where(a_at <= b_at, forward, backward) * pair_keep()
    return joined.reshape(lead + (CYL * CYL, FEEDS))


def body(samples, feed_input_wiring, input_flags):
    frames_here, inputs_here, length = samples.shape
    tm_parts = lax.axis_size("tm")
    wide_parts = lax.axis_size("wide")
    devices = tm_parts * wide_parts
    frames_all = frames_here * tm_parts
    local_channels = CH // devices
    table = channel_table_const(NSAMP, CH, CHAN_LO)
    chunks = math.gcd(2, local_channels)
    chunk_channels = local_channels // chunks
    table = table.reshape(devices, chunks, chunk_channels * 2, length).transpose(1, 0, 2, 3)
    table = jnp.asarray(table.reshape(chunks, devices * chunk_channels * 2, length), dtype=jnp.bfloat16)
    flattened = samples.reshape(frames_here * inputs_here, length)
    chunk_rows = devices * chunk_channels * 2
    table = table.reshape(chunks * chunk_rows, length)

    def channelize(rows):
        spectra = lax.dot_general(rows, flattened, NT, preferred_element_type=jnp.float32)
        return spectra.astype(jnp.bfloat16).reshape(-1, devices, chunk_channels, 2 * frames_here, inputs_here)

    spectra = [channelize(table[:chunk_rows])[0]]
    if chunks > 1:
        rest = channelize(table[chunk_rows:])
        spectra += [rest[j] for j in range(chunks - 1)]

    inputs_all = wide_parts * inputs_here
    flags = input_flags.astype(jnp.bfloat16)
    source = jnp.arange(inputs_all, dtype=jnp.int32)
    wiring_rev = jnp.flip(feed_input_wiring.reshape(CYL, FEEDS), axis=1).reshape(CYL * FEEDS)
    pt_full = jnp.where(feed_input_wiring[:, None] == source[None, :], flags[None, :], jnp.bfloat16(0))
    ptr_full = jnp.where(wiring_rev[:, None] == source[None, :], flags[None, :], jnp.bfloat16(0))
    first_lane = (lax.broadcasted_iota(jnp.int32, (CYL * FEEDS, 128), 1) == 0).astype(jnp.bfloat16)
    fm = jnp.sum(pt_full.astype(jnp.float32), axis=1).astype(jnp.bfloat16)[:, None] * first_lane
    fmr = jnp.sum(ptr_full.astype(jnp.float32), axis=1).astype(jnp.bfloat16)[:, None] * first_lane
    pt = pt_full.reshape(CYL * FEEDS, wide_parts, inputs_here).transpose(1, 0, 2)
    ptr = ptr_full.reshape(CYL * FEEDS, wide_parts, inputs_here).transpose(1, 0, 2)

    rows = tm_parts * 2 * frames_here
    r_at = np.arange(rows)
    frame_at = r_at % frames_here
    part_at = (r_at // frames_here) % 2
    group_at = r_at // (2 * frames_here)
    rm = np.zeros((rows, rows), np.float32)
    for r in range(rows):
        partner = group_at[r] * 2 * frames_here + (1 - part_at[r]) * frames_here + frame_at[r]
        rm[partner, r] = -1.0 if part_at[r] == 0 else 1.0
    rm = jnp.asarray(rm, dtype=jnp.bfloat16)

    sums = []
    for j in range(chunks):
        spectra_j = spectra[j]
        if j >= 2:
            spectra_j, _ = lax.optimization_barrier((spectra_j, sums[j - 2]))
        elif j == 1:
            spectra_j, pt, ptr, fm, fmr = lax.optimization_barrier((spectra_j, pt, ptr, fm, fmr))
        turned = lax.all_to_all(spectra_j, ("wide", "tm"), 0, 0, tiled=True)
        blk = turned.reshape(wide_parts, tm_parts, chunk_channels, 2 * frames_here, inputs_here)
        if j == 0:
            first, count_sums = correlate(blk, pt, ptr, rm, fm, fmr)
            sums.append(first)
        else:
            sums.append(correlate(blk, pt, ptr, rm)[0])
    sums = jnp.concatenate(sums, axis=0)
    conj_sign = jnp.array([1.0, -1.0], jnp.float32)[None, :, None, None, None]
    vis = unskew(sums, conj_sign)
    local_baselines = NBASE // devices
    send = vis.reshape(local_channels, 2, devices, local_baselines).transpose(2, 0, 1, 3)
    received = lax.all_to_all(send.astype(jnp.bfloat16), ("wide", "tm"), 0, 0, tiled=True)
    stacked_in = received.astype(jnp.float32).reshape(CH * 2, local_baselines)
    device_position = lax.axis_index("wide") * tm_parts + lax.axis_index("tm")
    global_stack_counts = unskew(count_sums, 1.0).reshape(NBASE)
    local_stack_counts = lax.dynamic_slice_in_dim(
        global_stack_counts, device_position * local_baselines, local_baselines
    )
    delay = delay_matrix_const(CH)
    spectra_out = lax.dot_general(
        stacked_in, delay, (((0,), (0,)), ((), ())), precision=lax.Precision.HIGH,
        preferred_element_type=jnp.float32,
    )
    weight = 1.0 / jnp.sqrt(frames_all * CH * jnp.maximum(local_stack_counts, 1.0))
    return spectra_out.reshape(local_baselines, 2, CH) * weight[:, None, None]


def solution(mesh):
    return jax.shard_map(
        body,
        mesh=mesh,
        in_specs=(P("tm", "wide", None), P(), P()),
        out_specs=P(("wide", "tm"), None, None),
        check_vma=False,
    )
```

```python
import functools
import math

import numpy as np
import jax
import jax.numpy as jnp
from jax import lax
from jax.experimental import pallas as pl
from jax.experimental.pallas import tpu as pltpu
from jax.sharding import PartitionSpec as P

CYL = 4
FEEDS = 256
NSAMP = 2048
CH = 512
CHAN_LO = 256
NBASE = 4096

NT = (((1,), (1,)), ((), ()))


def channel_table_const(length, frequency_channels, first):
    samples_at = np.arange(length, dtype=np.int64)
    channel_at = np.arange(frequency_channels, dtype=np.int64) + first
    turns = (channel_at[:, None] * samples_at[None, :]) % length
    phase = turns.astype(np.float32) * np.float32(2.0 * math.pi / length)
    scale = np.float32(1.0 / math.sqrt(length))
    both = np.stack([np.cos(phase) * scale, -np.sin(phase) * scale], axis=1)
    return both.reshape(2 * frequency_channels, length)


def delay_matrix_const(frequency_channels):
    index = np.arange(frequency_channels, dtype=np.int64)
    phase = ((index[:, None] * index[None, :]) % frequency_channels).astype(np.float32) * np.float32(
        2.0 * math.pi / frequency_channels
    )
    cosine = np.cos(phase).astype(np.float32)
    sine = np.sin(phase).astype(np.float32)
    w = np.zeros((frequency_channels, 2, 2, frequency_channels), np.float32)
    w[:, 0, 0] = cosine
    w[:, 1, 0] = sine
    w[:, 0, 1] = -sine
    w[:, 1, 1] = cosine
    return jnp.asarray(w.reshape(2 * frequency_channels, 2 * frequency_channels))


def pair_keep():
    same = jnp.eye(CYL, dtype=jnp.float32)[:, :, None]
    first = (jnp.arange(FEEDS, dtype=jnp.int32) == 0).astype(jnp.float32)[None, None, :]
    return 1.0 - same * first


HALF = FEEDS // 2


def diag_pairs(left, right, upper, upper_half, write):
    for a in range(CYL):
        for b in range(a, CYL):
            right_b = right[b * FEEDS:(b + 1) * FEEDS]
            if a == b:
                top = lax.dot_general(
                    left[a * FEEDS:a * FEEDS + HALF], right_b, NT, preferred_element_type=jnp.float32
                )
                top = pltpu.roll(top, 0, 1, stride=1, stride_axis=0)
                bottom = lax.dot_general(
                    left[a * FEEDS + HALF:(a + 1) * FEEDS], right_b[:HALF], NT,
                    preferred_element_type=jnp.float32,
                )
                bottom = pltpu.roll(bottom, 0, 1, stride=1, stride_axis=0)
                up_left = jnp.sum(jnp.where(upper_half, top[:, :HALF], 0.0), axis=0, keepdims=True)
                up_right = jnp.sum(top[:, HALF:], axis=0, keepdims=True) + jnp.sum(
                    jnp.where(upper_half, bottom, 0.0), axis=0, keepdims=True
                )
                write(a * CYL + b, jnp.concatenate([up_left, up_right], axis=1))
                continue
            tile = lax.dot_general(
                left[a * FEEDS:(a + 1) * FEEDS], right_b, NT, preferred_element_type=jnp.float32,
            )
            skewed = pltpu.roll(tile, 0, 1, stride=1, stride_axis=0)
            up = jnp.sum(jnp.where(upper, skewed, 0.0), axis=0, keepdims=True)
            write(a * CYL + b, up)
            total = jnp.sum(skewed, axis=0, keepdims=True)
            write(b * CYL + a, total - up)


def correlate_kernel(*refs, with_counts):
    if with_counts:
        x_ref, pt_ref, ptr_ref, rm_ref, fm_ref, fmr_ref, o_ref, n_ref = refs
    else:
        x_ref, pt_ref, ptr_ref, rm_ref, o_ref = refs
    wide_parts = x_ref.shape[0]
    row_at = lax.broadcasted_iota(jnp.int32, (FEEDS, FEEDS), 0)
    col_at = lax.broadcasted_iota(jnp.int32, (FEEDS, FEEDS), 1)
    upper = col_at >= row_at
    upper_half = upper[:HALF, :HALF]

    if with_counts:
        @pl.when(pl.program_id(0) == 0)
        def _():
            def write_count(slot, value):
                n_ref[pl.ds(slot, 1), :] = value

            diag_pairs(fm_ref[...], fmr_ref[...], upper, upper_half, write_count)

    g = None
    gr = None
    for w in range(wide_parts):
        xw = x_ref[w].reshape(-1, x_ref.shape[-1])
        gw = lax.dot_general(pt_ref[w], xw, NT, preferred_element_type=jnp.float32)
        grw = lax.dot_general(ptr_ref[w], xw, NT, preferred_element_type=jnp.float32)
        g = gw if g is None else g + gw
        gr = grw if gr is None else gr + grw
    g = g.astype(jnp.bfloat16)
    gr = gr.astype(jnp.bfloat16)
    yr = jnp.dot(gr, rm_ref[...], preferred_element_type=jnp.float32).astype(jnp.bfloat16)
    for part, right in enumerate((gr, yr)):
        def write_vis(slot, value, part=part):
            o_ref[0, part, pl.ds(slot, 1), :] = value

        diag_pairs(g, right, upper, upper_half, write_vis)


def counts_kernel(fm_ref, fmr_ref, n_ref):
    row_at = lax.broadcasted_iota(jnp.int32, (FEEDS, FEEDS), 0)
    col_at = lax.broadcasted_iota(jnp.int32, (FEEDS, FEEDS), 1)
    upper = col_at >= row_at

    def write_count(slot, value):
        n_ref[pl.ds(slot, 1), :] = value

    diag_pairs(fm_ref[...], fmr_ref[...], upper, upper[:HALF, :HALF], write_count)


def stack_counts(fm, fmr):
    return pl.pallas_call(
        counts_kernel,
        out_shape=jax.ShapeDtypeStruct((CYL * CYL, FEEDS), jnp.float32),
    )(fm, fmr)


def correlate(blocks, pt, ptr, rm, fm=None, fmr=None):
    wide_parts, tm_parts, local_channels, rows_each, inputs_each = blocks.shape
    with_counts = fm is not None
    in_specs = [
        pl.BlockSpec((wide_parts, tm_parts, None, rows_each, inputs_each), lambda c: (0, 0, c, 0, 0)),
        pl.BlockSpec(pt.shape, lambda c: (0, 0, 0)),
        pl.BlockSpec(ptr.shape, lambda c: (0, 0, 0)),
        pl.BlockSpec(rm.shape, lambda c: (0, 0)),
    ]
    out_specs = [pl.BlockSpec((1, 2, CYL * CYL, FEEDS), lambda c: (c, 0, 0, 0))]
    out_shape = [jax.ShapeDtypeStruct((local_channels, 2, CYL * CYL, FEEDS), jnp.float32)]
    operands = [blocks, pt, ptr, rm]
    if with_counts:
        in_specs += [pl.BlockSpec(fm.shape, lambda c: (0, 0)), pl.BlockSpec(fmr.shape, lambda c: (0, 0))]
        out_specs.append(pl.BlockSpec((CYL * CYL, FEEDS), lambda c: (0, 0)))
        out_shape.append(jax.ShapeDtypeStruct((CYL * CYL, FEEDS), jnp.float32))
        operands += [fm, fmr]
    positions = CYL * FEEDS
    rows = tm_parts * rows_each
    flops = local_channels * (
        2 * 2 * positions * wide_parts * inputs_each * rows + 2 * positions * rows * rows
        + 20 * 2 * FEEDS * FEEDS * rows
    )
    bytes_accessed = blocks.size * 2 + pt.size * 4 + local_channels * 2 * CYL * CYL * FEEDS * 4
    return pl.pallas_call(
        functools.partial(correlate_kernel, with_counts=with_counts),
        grid=(local_channels,),
        in_specs=in_specs,
        out_specs=out_specs,
        out_shape=out_shape,
        cost_estimate=pl.CostEstimate(flops=flops, transcendentals=0, bytes_accessed=bytes_accessed),
    )(*operands)


def unskew(sums, sign):
    lead = sums.shape[:-2]
    grid = sums.reshape(lead + (CYL, CYL, FEEDS))
    forward = jnp.flip(grid, axis=-1)
    shifted = jnp.roll(grid, 1, axis=-1)
    first_of_pair = jnp.swapaxes(forward, -3, -2)[..., :1]
    k_at = lax.broadcasted_iota(jnp.int32, (CYL, CYL, FEEDS), 2)
    a_at = lax.broadcasted_iota(jnp.int32, (CYL, CYL, FEEDS), 0)
    b_at = lax.broadcasted_iota(jnp.int32, (CYL, CYL, FEEDS), 1)
    backward = jnp.where(k_at == 0, first_of_pair, shifted) * sign
    joined = jnp.where(a_at <= b_at, forward, backward) * pair_keep()
    return joined.reshape(lead + (CYL * CYL, FEEDS))


def body(samples, feed_input_wiring, input_flags):
    frames_here, inputs_here, length = samples.shape
    tm_parts = lax.axis_size("tm")
    wide_parts = lax.axis_size("wide")
    devices = tm_parts * wide_parts
    frames_all = frames_here * tm_parts
    local_channels = CH // devices
    table = channel_table_const(NSAMP, CH, CHAN_LO)
    chunks = math.gcd(2, local_channels)
    chunk_channels = local_channels // chunks
    table = table.reshape(devices, chunks, chunk_channels * 2, length).transpose(1, 0, 2, 3)
    table = jnp.asarray(table.reshape(chunks, devices * chunk_channels * 2, length), dtype=jnp.bfloat16)
    flattened = samples.reshape(frames_here * inputs_here, length)
    chunk_rows = devices * chunk_channels * 2
    table = table.reshape(chunks * chunk_rows, length)

    def channelize(rows):
        spectra = lax.dot_general(rows, flattened, NT, preferred_element_type=jnp.float32)
        return spectra.astype(jnp.bfloat16).reshape(-1, devices, chunk_channels, 2 * frames_here, inputs_here)

    spectra = [channelize(table[:chunk_rows])[0]]
    if chunks > 1:
        rest = channelize(table[chunk_rows:])
        spectra += [rest[j] for j in range(chunks - 1)]

    inputs_all = wide_parts * inputs_here
    flags = input_flags.astype(jnp.bfloat16)
    source = jnp.arange(inputs_all, dtype=jnp.int32)
    wiring_rev = jnp.flip(feed_input_wiring.reshape(CYL, FEEDS), axis=1).reshape(CYL * FEEDS)
    pt_full = jnp.where(feed_input_wiring[:, None] == source[None, :], flags[None, :], jnp.bfloat16(0))
    ptr_full = jnp.where(wiring_rev[:, None] == source[None, :], flags[None, :], jnp.bfloat16(0))
    first_lane = (lax.broadcasted_iota(jnp.int32, (CYL * FEEDS, 128), 1) == 0).astype(jnp.bfloat16)
    fm = jnp.sum(pt_full.astype(jnp.float32), axis=1).astype(jnp.bfloat16)[:, None] * first_lane
    fmr = jnp.sum(ptr_full.astype(jnp.float32), axis=1).astype(jnp.bfloat16)[:, None] * first_lane
    pt = pt_full.reshape(CYL * FEEDS, wide_parts, inputs_here).transpose(1, 0, 2)
    ptr = ptr_full.reshape(CYL * FEEDS, wide_parts, inputs_here).transpose(1, 0, 2)

    rows = tm_parts * 2 * frames_here
    r_at = np.arange(rows)
    frame_at = r_at % frames_here
    part_at = (r_at // frames_here) % 2
    group_at = r_at // (2 * frames_here)
    rm = np.zeros((rows, rows), np.float32)
    for r in range(rows):
        partner = group_at[r] * 2 * frames_here + (1 - part_at[r]) * frames_here + frame_at[r]
        rm[partner, r] = -1.0 if part_at[r] == 0 else 1.0
    rm = jnp.asarray(rm, dtype=jnp.bfloat16)

    count_sums = stack_counts(fm, fmr)
    sums = []
    for j in range(chunks):
        spectra_j = spectra[j]
        if j >= 2:
            spectra_j, _ = lax.optimization_barrier((spectra_j, sums[j - 2]))
        elif j == 1:
            spectra_j, pt, ptr, count_sums = lax.optimization_barrier((spectra_j, pt, ptr, count_sums))
        turned = lax.all_to_all(spectra_j, ("wide", "tm"), 0, 0, tiled=True)
        blk = turned.reshape(wide_parts, tm_parts, chunk_channels, 2 * frames_here, inputs_here)
        sums.append(correlate(blk, pt, ptr, rm)[0])
    sums = jnp.concatenate(sums, axis=0)
    conj_sign = jnp.array([1.0, -1.0], jnp.float32)[None, :, None, None, None]
    vis = unskew(sums, conj_sign)
    local_baselines = NBASE // devices
    send = vis.reshape(local_channels, 2, devices, local_baselines).transpose(2, 0, 1, 3)
    received = lax.all_to_all(send.astype(jnp.bfloat16), ("wide", "tm"), 0, 0, tiled=True)
    stacked_in = received.astype(jnp.float32).reshape(CH * 2, local_baselines)
    device_position = lax.axis_index("wide") * tm_parts + lax.axis_index("tm")
    global_stack_counts = unskew(count_sums, 1.0).reshape(NBASE)
    local_stack_counts = lax.dynamic_slice_in_dim(
        global_stack_counts, device_position * local_baselines, local_baselines
    )
    delay = delay_matrix_const(CH)
    spectra_out = lax.dot_general(
        stacked_in, delay, (((0,), (0,)), ((), ())), precision=lax.Precision.HIGH,
        preferred_element_type=jnp.float32,
    )
    weight = 1.0 / jnp.sqrt(frames_all * CH * jnp.maximum(local_stack_counts, 1.0))
    return spectra_out.reshape(local_baselines, 2, CH) * weight[:, None, None]


def solution(mesh):
    return jax.shard_map(
        body,
        mesh=mesh,
        in_specs=(P("tm", "wide", None), P(), P()),
        out_specs=P(("wide", "tm"), None, None),
        check_vma=False,
    )
```

```python
import functools
import math

import numpy as np
import jax
import jax.numpy as jnp
from jax import lax
from jax.experimental import pallas as pl
from jax.experimental.pallas import tpu as pltpu
from jax.sharding import PartitionSpec as P

CYL = 4
FEEDS = 256
NSAMP = 2048
CH = 512
CHAN_LO = 256
NBASE = 4096

NT = (((1,), (1,)), ((), ()))


def channel_table_const(length, frequency_channels, first):
    samples_at = np.arange(length, dtype=np.int64)
    channel_at = np.arange(frequency_channels, dtype=np.int64) + first
    turns = (channel_at[:, None] * samples_at[None, :]) % length
    phase = turns.astype(np.float32) * np.float32(2.0 * math.pi / length)
    scale = np.float32(1.0 / math.sqrt(length))
    both = np.stack([np.cos(phase) * scale, -np.sin(phase) * scale], axis=1)
    return both.reshape(2 * frequency_channels, length)


def delay_matrix_const(frequency_channels):
    index = np.arange(frequency_channels, dtype=np.int64)
    phase = ((index[:, None] * index[None, :]) % frequency_channels).astype(np.float32) * np.float32(
        2.0 * math.pi / frequency_channels
    )
    cosine = np.cos(phase).astype(np.float32)
    sine = np.sin(phase).astype(np.float32)
    w = np.zeros((frequency_channels, 2, 2, frequency_channels), np.float32)
    w[:, 0, 0] = cosine
    w[:, 1, 0] = sine
    w[:, 0, 1] = -sine
    w[:, 1, 1] = cosine
    return jnp.asarray(w.reshape(2 * frequency_channels, 2 * frequency_channels))


def pair_keep():
    same = jnp.eye(CYL, dtype=jnp.float32)[:, :, None]
    first = (jnp.arange(FEEDS, dtype=jnp.int32) == 0).astype(jnp.float32)[None, None, :]
    return 1.0 - same * first


HALF = FEEDS // 2


def diag_pairs(left, right, upper, upper_half, write):
    for a in range(CYL):
        for b in range(a, CYL):
            right_b = right[b * FEEDS:(b + 1) * FEEDS]
            if a == b:
                top = lax.dot_general(
                    left[a * FEEDS:a * FEEDS + HALF], right_b, NT, preferred_element_type=jnp.float32
                )
                top = pltpu.roll(top, 0, 1, stride=1, stride_axis=0)
                bottom = lax.dot_general(
                    left[a * FEEDS + HALF:(a + 1) * FEEDS], right_b[:HALF], NT,
                    preferred_element_type=jnp.float32,
                )
                bottom = pltpu.roll(bottom, 0, 1, stride=1, stride_axis=0)
                up_left = jnp.sum(jnp.where(upper_half, top[:, :HALF], 0.0), axis=0, keepdims=True)
                up_right = jnp.sum(top[:, HALF:], axis=0, keepdims=True) + jnp.sum(
                    jnp.where(upper_half, bottom, 0.0), axis=0, keepdims=True
                )
                write(a * CYL + b, jnp.concatenate([up_left, up_right], axis=1))
                continue
            tile = lax.dot_general(
                left[a * FEEDS:(a + 1) * FEEDS], right_b, NT, preferred_element_type=jnp.float32,
            )
            skewed = pltpu.roll(tile, 0, 1, stride=1, stride_axis=0)
            up = jnp.sum(jnp.where(upper, skewed, 0.0), axis=0, keepdims=True)
            write(a * CYL + b, up)
            total = jnp.sum(skewed, axis=0, keepdims=True)
            write(b * CYL + a, total - up)


def correlate_kernel(*refs, with_counts):
    if with_counts:
        x_ref, pt_ref, ptr_ref, rm_ref, fm_ref, fmr_ref, o_ref, n_ref = refs
    else:
        x_ref, pt_ref, ptr_ref, rm_ref, o_ref = refs
    wide_parts = x_ref.shape[0]
    row_at = lax.broadcasted_iota(jnp.int32, (FEEDS, FEEDS), 0)
    col_at = lax.broadcasted_iota(jnp.int32, (FEEDS, FEEDS), 1)
    upper = col_at >= row_at
    upper_half = upper[:HALF, :HALF]

    if with_counts:
        @pl.when(pl.program_id(0) == 0)
        def _():
            def write_count(slot, value):
                n_ref[pl.ds(slot, 1), :] = value

            diag_pairs(fm_ref[...], fmr_ref[...], upper, upper_half, write_count)

    g = None
    gr = None
    for w in range(wide_parts):
        xw = x_ref[w].reshape(-1, x_ref.shape[-1])
        gw = lax.dot_general(pt_ref[w], xw, NT, preferred_element_type=jnp.float32)
        grw = lax.dot_general(ptr_ref[w], xw, NT, preferred_element_type=jnp.float32)
        g = gw if g is None else g + gw
        gr = grw if gr is None else gr + grw
    g = g.astype(jnp.bfloat16)
    gr = gr.astype(jnp.bfloat16)
    yr = jnp.dot(gr, rm_ref[...], preferred_element_type=jnp.float32).astype(jnp.bfloat16)
    for part, right in enumerate((gr, yr)):
        def write_vis(slot, value, part=part):
            o_ref[0, part, pl.ds(slot, 1), :] = value

        diag_pairs(g, right, upper, upper_half, write_vis)


def counts_kernel(fm_ref, fmr_ref, n_ref):
    row_at = lax.broadcasted_iota(jnp.int32, (FEEDS, FEEDS), 0)
    col_at = lax.broadcasted_iota(jnp.int32, (FEEDS, FEEDS), 1)
    upper = col_at >= row_at

    def write_count(slot, value):
        n_ref[pl.ds(slot, 1), :] = value

    diag_pairs(fm_ref[...], fmr_ref[...], upper, upper[:HALF, :HALF], write_count)


def stack_counts(fm, fmr):
    return pl.pallas_call(
        counts_kernel,
        out_shape=jax.ShapeDtypeStruct((CYL * CYL, FEEDS), jnp.float32),
    )(fm, fmr)


def correlate(blocks, pt, ptr, rm, fm=None, fmr=None):
    wide_parts, tm_parts, local_channels, rows_each, inputs_each = blocks.shape
    with_counts = fm is not None
    in_specs = [
        pl.BlockSpec((wide_parts, tm_parts, None, rows_each, inputs_each), lambda c: (0, 0, c, 0, 0)),
        pl.BlockSpec(pt.shape, lambda c: (0, 0, 0)),
        pl.BlockSpec(ptr.shape, lambda c: (0, 0, 0)),
        pl.BlockSpec(rm.shape, lambda c: (0, 0)),
    ]
    out_specs = [pl.BlockSpec((1, 2, CYL * CYL, FEEDS), lambda c: (c, 0, 0, 0))]
    out_shape = [jax.ShapeDtypeStruct((local_channels, 2, CYL * CYL, FEEDS), jnp.float32)]
    operands = [blocks, pt, ptr, rm]
    if with_counts:
        in_specs += [pl.BlockSpec(fm.shape, lambda c: (0, 0)), pl.BlockSpec(fmr.shape, lambda c: (0, 0))]
        out_specs.append(pl.BlockSpec((CYL * CYL, FEEDS), lambda c: (0, 0)))
        out_shape.append(jax.ShapeDtypeStruct((CYL * CYL, FEEDS), jnp.float32))
        operands += [fm, fmr]
    positions = CYL * FEEDS
    rows = tm_parts * rows_each
    flops = local_channels * (
        2 * 2 * positions * wide_parts * inputs_each * rows + 2 * positions * rows * rows
        + 20 * 2 * FEEDS * FEEDS * rows
    )
    bytes_accessed = blocks.size * 2 + pt.size * 4 + local_channels * 2 * CYL * CYL * FEEDS * 4
    return pl.pallas_call(
        functools.partial(correlate_kernel, with_counts=with_counts),
        grid=(local_channels,),
        in_specs=in_specs,
        out_specs=out_specs,
        out_shape=out_shape,
        cost_estimate=pl.CostEstimate(flops=flops, transcendentals=0, bytes_accessed=bytes_accessed),
    )(*operands)


def unskew(sums, sign):
    lead = sums.shape[:-2]
    grid = sums.reshape(lead + (CYL, CYL, FEEDS))
    forward = jnp.flip(grid, axis=-1)
    shifted = jnp.roll(grid, 1, axis=-1)
    first_of_pair = jnp.swapaxes(forward, -3, -2)[..., :1]
    k_at = lax.broadcasted_iota(jnp.int32, (CYL, CYL, FEEDS), 2)
    a_at = lax.broadcasted_iota(jnp.int32, (CYL, CYL, FEEDS), 0)
    b_at = lax.broadcasted_iota(jnp.int32, (CYL, CYL, FEEDS), 1)
    backward = jnp.where(k_at == 0, first_of_pair, shifted) * sign
    joined = jnp.where(a_at <= b_at, forward, backward) * pair_keep()
    return joined.reshape(lead + (CYL * CYL, FEEDS))


def body(samples, feed_input_wiring, input_flags):
    frames_here, inputs_here, length = samples.shape
    tm_parts = lax.axis_size("tm")
    wide_parts = lax.axis_size("wide")
    devices = tm_parts * wide_parts
    frames_all = frames_here * tm_parts
    local_channels = CH // devices
    table = channel_table_const(NSAMP, CH, CHAN_LO)
    chunks = math.gcd(2, local_channels)
    chunk_channels = local_channels // chunks
    table = table.reshape(devices, chunks, chunk_channels * 2, length).transpose(1, 0, 2, 3)
    table = jnp.asarray(table.reshape(chunks, devices * chunk_channels * 2, length), dtype=jnp.bfloat16)
    flattened = samples.reshape(frames_here * inputs_here, length)
    chunk_rows = devices * chunk_channels * 2
    table = table.reshape(chunks * chunk_rows, length)

    def channelize(rows):
        spectra = lax.dot_general(rows, flattened, NT, preferred_element_type=jnp.float32)
        return spectra.astype(jnp.bfloat16).reshape(-1, devices, chunk_channels, 2 * frames_here, inputs_here)

    spectra = [channelize(table[:chunk_rows])[0]]
    if chunks > 1:
        rest = channelize(table[chunk_rows:])
        spectra += [rest[j] for j in range(chunks - 1)]

    inputs_all = wide_parts * inputs_here
    flags = input_flags.astype(jnp.bfloat16)
    source = jnp.arange(inputs_all, dtype=jnp.int32)
    wiring_rev = jnp.flip(feed_input_wiring.reshape(CYL, FEEDS), axis=1).reshape(CYL * FEEDS)
    pt_full = jnp.where(feed_input_wiring[:, None] == source[None, :], flags[None, :], jnp.bfloat16(0))
    ptr_full = jnp.where(wiring_rev[:, None] == source[None, :], flags[None, :], jnp.bfloat16(0))
    first_lane = (lax.broadcasted_iota(jnp.int32, (CYL * FEEDS, 128), 1) == 0).astype(jnp.bfloat16)
    fm = jnp.sum(pt_full.astype(jnp.float32), axis=1).astype(jnp.bfloat16)[:, None] * first_lane
    fmr = jnp.sum(ptr_full.astype(jnp.float32), axis=1).astype(jnp.bfloat16)[:, None] * first_lane
    pt = pt_full.reshape(CYL * FEEDS, wide_parts, inputs_here).transpose(1, 0, 2)
    ptr = ptr_full.reshape(CYL * FEEDS, wide_parts, inputs_here).transpose(1, 0, 2)

    rows = tm_parts * 2 * frames_here
    r_at = np.arange(rows)
    frame_at = r_at % frames_here
    part_at = (r_at // frames_here) % 2
    group_at = r_at // (2 * frames_here)
    rm = np.zeros((rows, rows), np.float32)
    for r in range(rows):
        partner = group_at[r] * 2 * frames_here + (1 - part_at[r]) * frames_here + frame_at[r]
        rm[partner, r] = -1.0 if part_at[r] == 0 else 1.0
    rm = jnp.asarray(rm, dtype=jnp.bfloat16)

    count_sums = stack_counts(fm, fmr)
    sums = []
    for j in range(chunks):
        spectra_j = spectra[j]
        if j >= 2:
            spectra_j, _ = lax.optimization_barrier((spectra_j, sums[j - 2]))
        elif j == 1:
            spectra_j, pt, ptr, count_sums = lax.optimization_barrier((spectra_j, pt, ptr, count_sums))
        turned = lax.all_to_all(spectra_j, ("wide", "tm"), 0, 0, tiled=True)
        blk = turned.reshape(wide_parts, tm_parts, chunk_channels, 2 * frames_here, inputs_here)
        sums.append(correlate(blk, pt, ptr, rm)[0])
    sums = jnp.concatenate(sums, axis=0)
    conj_sign = jnp.array([1.0, -1.0], jnp.float32)[None, :, None, None, None]
    vis = unskew(sums, conj_sign)
    local_baselines = NBASE // devices
    send = vis.reshape(local_channels, 2, devices, local_baselines).transpose(2, 0, 1, 3)
    received = lax.all_to_all(send.astype(jnp.bfloat16), ("wide", "tm"), 0, 0, tiled=True)
    stacked_in = received.reshape(CH * 2, local_baselines)
    device_position = lax.axis_index("wide") * tm_parts + lax.axis_index("tm")
    global_stack_counts = unskew(count_sums, 1.0).reshape(NBASE)
    local_stack_counts = lax.dynamic_slice_in_dim(
        global_stack_counts, device_position * local_baselines, local_baselines
    )
    delay = delay_matrix_const(CH).astype(jnp.bfloat16)
    spectra_out = lax.dot_general(
        stacked_in, delay, (((0,), (0,)), ((), ())), preferred_element_type=jnp.float32,
    )
    weight = 1.0 / jnp.sqrt(frames_all * CH * jnp.maximum(local_stack_counts, 1.0))
    return spectra_out.reshape(local_baselines, 2, CH) * weight[:, None, None]


def solution(mesh):
    return jax.shard_map(
        body,
        mesh=mesh,
        in_specs=(P("tm", "wide", None), P(), P()),
        out_specs=P(("wide", "tm"), None, None),
        check_vma=False,
    )
```
